32 devices in a mesh: attn: 8 (over z, y), exp: 4 (over x, core).
Axes of the slice: x: 2, y: 2, z: 4, core: 2. Of those that a mesh axis runs over, the one named last changes fastest.
Arguments:
- patches: bfloat16 [1536, 4096], P('attn', 'exp'), may hold values from -6 to 6
- grad_out: bfloat16 [1536, 4096], P('attn', 'exp'), may hold values from -6 to 6
- route_ids: int32 [1536, 2], P('attn'), may hold values from 0 to 15, all different within a row; in each aligned block of 192 rows (0 to 191, 192 to 383, ...) at most 48 rows name the same one
- gates: float32 [1536, 2], P('attn'), may hold values from 0.25 to 1
- w_up: bfloat16 [32, 4096, 768], P(('attn', 'exp')), may hold values from -0.09375 to 0.09375
- w_down: bfloat16 [32, 768, 4096], P(('attn', 'exp')), may hold values from -0.15625 to 0.15625
Outputs:
- mixed: bfloat16 [1536, 4096], P('attn', 'exp')
- grad_patches: bfloat16 [1536, 4096], P('attn', 'exp')
- grad_up: float32 [32, 4096, 768], P(('attn', 'exp'))
- grad_down: float32 [32, 768, 4096], P(('attn', 'exp'))
The draws below stay inside these ranges and needn't reach their ends.
Inputs may be any that keep to these rules, and one draw needn't show every extreme that they name: `route_ids`: the two experts of a row differ; among the 192 rows of one index of attn, no expert is named by more than 48 rows, a bound that some block reaches.
All inputs are finite; a program needn't handle non-finite values.
Results may differ from the reference program's by a relative error of at most 0.0064.
Values may be sent and summed in bfloat16 or wider, within the bound.
No kernel may reach another device: no remote copies, remote signals or barrier semaphores. Data moves between devices by JAX's collectives and lax.ppermute only.
A program may use at most 128 MiB of HBM per device.

```python
import math
import jax
import jax.numpy as jnp
import numpy as np
from jax import lax

D = 4096
HID = 1536
EXP_DEV = 2
TOK_SEC = 192
EXPERTS = 16
GROUPS = 2
HID_DEV = 768
CAP = 48
TOKENS = 1536
N_ATTN = 8
N_EXP = 4


def steps_of(key, shape, cuts, least, top_value):
    level = 1.0
    for position, blocks in cuts:
        draws = jax.random.uniform(jax.random.fold_in(jax.random.fold_in(key, 6), position), (blocks,), jnp.float32, least / len(cuts), top_value / len(cuts))
        level = level * jnp.repeat(jnp.exp(draws), shape[position] // blocks).reshape((-1,) + (1,) * (len(shape) - 1 - position))
    return level


def deal_out(stream_key, own, number, rows, number_of, top, reach, lean):
    sequence = jax.random.permutation(stream_key, number_of)
    crowded, ordinary = shares(number_of, rows * top, reach, lean, True), shares(number_of, rows * top, reach, lean, False)
    places = jnp.arange(number_of)

    def named(tallies, offset_by):
        used = int((tallies > 0).sum())
        fixed = max(1, used // 4)
        passed = fixed + (places - fixed + offset_by * (used - fixed)) % max(1, number_of - fixed)
        return jnp.zeros((number_of,), jnp.int32).at[sequence[jnp.where(places < fixed, places, passed)]].set(jnp.asarray(tallies, jnp.int32))

    tallies = jnp.where(number % 4 == 0, named(crowded, number // 4), named(ordinary, number - number // 4 - 1))
    mixed = jax.random.permutation(jax.random.fold_in(own, 3), number_of)
    donor, taker = mixed[0:number_of // 2 * 2:2], mixed[1:number_of // 2 * 2:2]
    slack = jnp.minimum(tallies[donor] - 1, reach - tallies[taker]) // 2
    slack = jnp.where((donor == sequence[0]) | (taker == sequence[0]) | (tallies[taker] == 0), 0, jnp.maximum(slack, 0))
    passed = jax.random.randint(jax.random.fold_in(own, 4), (number_of // 2,), 0, 1 << 20) % (slack + 1)
    tallies = tallies.at[donor].add(-passed).at[taker].add(passed)
    members = jnp.searchsorted(jnp.cumsum(tallies), jnp.arange(rows * top), side="right").astype(jnp.int32)
    grid = members.reshape(top, rows).T
    grid = grid[jax.random.permutation(jax.random.fold_in(own, 1), rows)]
    offset_by = jax.random.randint(jax.random.fold_in(own, 2), (rows, 1), 0, top)
    return jnp.take_along_axis(grid, (jnp.arange(top)[None, :] + offset_by) % top, axis=1)


def shares(number_of, total, most, skew, full):
    weights = [(1 << 20) // math.isqrt(rank ** skew) + 1 for rank in range(1, number_of + 1)]
    largest = most if full else min(most, max(-(-total // number_of), total * weights[0] // sum(weights)))
    least = 1 if total - largest >= number_of - 1 else 0
    holding, surplus = [largest] + [least] * (number_of - 1), total - largest - least * (number_of - 1)
    while surplus > 0:
        free = [i for i in range(1, number_of) if holding[i] < largest] or [i for i in range(1, number_of) if holding[i] < most]
        pool, left = sum([weights[i] for i in free]), surplus
        for i in free:
            extra = min(most - holding[i], max(1, left * weights[i] // pool), surplus)
            holding[i] = holding[i] + extra
            surplus = surplus - extra
    return np.array(holding)


def centred(rng, dims, width, reach, shards=(), kind=jnp.bfloat16):
    level = steps_of(rng, dims, shards, -0.22, 0.18) if shards else 1.0
    result = jax.random.normal(rng, dims, jnp.float32) * width * level
    return jnp.minimum(jnp.maximum(result, -reach), reach).astype(kind)


def setup_inputs(seed: int = 0) -> dict:
    keys = jax.random.split(jax.random.key(seed), 7)
    patches = centred(keys[0], (TOKENS, D), 1.0, 6.0, ((0, 8), (1, 4)))
    grad_out = centred(keys[1], (TOKENS, D), 1.0, 6.0, ((0, 8), (1, 4)))
    route_ids_keys = jax.random.split(jax.random.fold_in(keys[2], 1), TOKENS // TOK_SEC)
    route_ids_turns = jax.random.permutation(jax.random.fold_in(keys[2], 3), TOKENS // TOK_SEC)
    route_ids = jax.vmap(lambda own, number: deal_out(jax.random.fold_in(keys[2], 2), own, number, TOK_SEC, EXPERTS, 2, CAP, 2))(route_ids_keys, route_ids_turns).reshape((TOKENS, 2))
    gates = jnp.clip(0.25 + 0.75 * jax.random.uniform(keys[3], (TOKENS, 2), jnp.float32) ** steps_of(keys[3], (TOKENS, 2), ((0, 8),), -0.2, 0.2), 0.25, 1.0)
    w_up = centred(keys[4], (EXPERTS * GROUPS, D, HID_DEV), D ** -0.5, 0.09375, ((0, 32),))
    w_down = centred(keys[5], (EXPERTS * GROUPS, HID_DEV, D), HID ** -0.5, 0.15625, ((0, 32),))
    return {"patches": patches, "grad_out": grad_out, "route_ids": route_ids, "gates": gates, "w_up": w_up, "w_down": w_down}


def gelu_parts(pre_act):
    inner_arg = 0.7978845608 * (pre_act + 0.044715 * pre_act * pre_act * pre_act)
    tanh_val = jnp.tanh(inner_arg)
    gelu_value = 0.5 * pre_act * (1.0 + tanh_val)
    gelu_slope = 0.5 * (1.0 + tanh_val) + 0.5 * pre_act * (1.0 - tanh_val * tanh_val) * 0.7978845608 * (1.0 + 0.134145 * pre_act * pre_act)
    return gelu_value, gelu_slope


def group_sum(parts):
    rounded = lax.optimization_barrier(parts.astype(jnp.bfloat16))
    return jnp.sum(rounded.astype(jnp.float32), axis=0)


def reference(patches, grad_out, route_ids, gates, w_up, w_down):
    feat_width = patches.shape[1]
    per_expert = N_ATTN * CAP
    groups = N_EXP // EXP_DEV
    hid_dev = HID // groups
    assign_count = TOKENS * 2
    sec_ids = route_ids.reshape(N_ATTN, TOK_SEC * 2).astype(jnp.int32)
    one_hot = (sec_ids[:, :, None] == jnp.arange(EXPERTS, dtype=jnp.int32)[None, None, :]).astype(jnp.int32)
    before = jnp.cumsum(one_hot, axis=1) - one_hot
    rank_in = jnp.sum(before * one_hot, axis=2)
    section = jnp.arange(N_ATTN, dtype=jnp.int32)[:, None]
    slot_ids = (sec_ids * per_expert + section * CAP + rank_in).reshape(-1).astype(jnp.int32)
    slot_table = jnp.full((EXPERTS * per_expert,), assign_count, jnp.int32).at[slot_ids].set(jnp.arange(assign_count, dtype=jnp.int32))
    slot_table = slot_table.reshape(EXPERTS, per_expert)
    dout = (gates[:, :, None] * grad_out[:, None, :].astype(jnp.float32)).astype(jnp.bfloat16).reshape(assign_count, feat_width)
    blank_row = jnp.zeros((1, feat_width), jnp.bfloat16)
    x_pad = jnp.concatenate([jnp.repeat(patches, 2, axis=0), blank_row], axis=0)
    d_pad = jnp.concatenate([dout, blank_row], axis=0)
    up_all = w_up.reshape(EXPERTS, groups, feat_width, hid_dev)
    down_all = w_down.reshape(EXPERTS, groups, hid_dev, feat_width)

    def per_expert_work(expert_item):
        row_index, up_groups, down_groups = expert_item
        up_mat = jnp.transpose(up_groups, (1, 0, 2)).reshape(feat_width, HID)
        down_mat = down_groups.reshape(HID, feat_width)
        x_rows = x_pad[row_index]
        d_rows = d_pad[row_index]
        pre_act = jnp.dot(x_rows, up_mat, preferred_element_type=jnp.float32)
        gelu_value, gelu_slope = gelu_parts(pre_act)
        activation = gelu_value.astype(jnp.bfloat16)
        act_groups = activation.astype(jnp.float32).reshape(per_expert, groups, hid_dev)
        out_rows = group_sum(jnp.einsum('mgh,ghd->gmd', act_groups, down_groups.astype(jnp.float32)))
        grad_act = jnp.dot(d_rows, down_mat.T, preferred_element_type=jnp.float32)
        grad_pre = (grad_act * gelu_slope).astype(jnp.bfloat16)
        grad_downmat = jnp.dot(activation.T, d_rows, preferred_element_type=jnp.float32).reshape(groups, hid_dev, feat_width)
        grad_upmat = jnp.dot(x_rows.T, grad_pre, preferred_element_type=jnp.float32)
        grad_upmat = jnp.transpose(grad_upmat.reshape(feat_width, groups, hid_dev), (1, 0, 2))
        pre_groups = grad_pre.astype(jnp.float32).reshape(per_expert, groups, hid_dev)
        dx_rows = group_sum(jnp.einsum('mgh,gdh->gmd', pre_groups, up_groups.astype(jnp.float32)))
        return out_rows, dx_rows, grad_upmat, grad_downmat

    out_all, dx_all, grad_up, grad_down = lax.map(per_expert_work, (slot_table, up_all, down_all))
    picked_out = out_all.reshape(-1, feat_width)[slot_ids].reshape(TOKENS, 2, feat_width)
    picked_dx = dx_all.reshape(-1, feat_width)[slot_ids].reshape(TOKENS, 2, feat_width)
    mixed = jnp.sum(gates[:, :, None] * picked_out, axis=1).astype(jnp.bfloat16)
    grad_patches = jnp.sum(picked_dx, axis=1).astype(jnp.bfloat16)
    grad_up = grad_up.reshape(EXPERTS * groups, feat_width, hid_dev)
    grad_down = grad_down.reshape(EXPERTS * groups, hid_dev, feat_width)
    return (mixed, grad_patches, grad_up, grad_down)
```

```python
import jax
import jax.numpy as jnp
from jax import lax
from jax.sharding import PartitionSpec as P

EXP_DEV = 2


def gelu_parts(pre_act):
    inner_arg = 0.7978845608 * (pre_act + 0.044715 * pre_act * pre_act * pre_act)
    tanh_val = jnp.tanh(inner_arg)
    gelu_value = 0.5 * pre_act * (1.0 + tanh_val)
    gelu_slope = 0.5 * (1.0 + tanh_val) + 0.5 * pre_act * (
        1.0 - tanh_val * tanh_val
    ) * 0.7978845608 * (1.0 + 0.134145 * pre_act * pre_act)
    return (gelu_value, gelu_slope)


def route_slots(route_ids, experts, capacity):
    flat_ids = route_ids.reshape(-1)
    one_hot = (flat_ids[:, None] == jnp.arange(experts, dtype=jnp.int32)[None, :]).astype(jnp.int32)
    before = jnp.cumsum(one_hot, axis=0) - one_hot
    rank_in = jnp.sum(before * one_hot, axis=1).reshape(route_ids.shape)
    return (route_ids // EXP_DEV) * capacity + rank_in


def on_device(patches, grad_out, route_ids, gates, w_up, w_down):
    sections = lax.axis_size("attn")
    n_exp = lax.axis_size("exp")
    cores = n_exp // EXP_DEV
    me = lax.axis_index("exp")
    half = me // cores
    core = me % cores
    experts = EXP_DEV * sections
    token_count, slice_w = patches.shape
    capacity = 4 * token_count // experts
    slots = sections * capacity
    n_loc, model_width, hid_loc = w_up.shape
    sub_w = EXP_DEV * slice_w
    f32 = jnp.float32
    bf16 = jnp.bfloat16

    def core_shift(s):
        return [(i, (i // cores) * cores + (i % cores + s) % cores) for i in range(n_exp)]

    half_swap = [(i, (i + cores) % n_exp) for i in range(n_exp)]

    def core_subset(local):
        other = lax.ppermute(local, "exp", half_swap)
        first = half == 0
        return jnp.concatenate(
            [jnp.where(first, local, other), jnp.where(first, other, local)], axis=1
        )

    sub_x = core_subset(patches)
    sub_dy = core_subset(grad_out)

    local_slot = route_slots(route_ids, experts, capacity)
    owned = (route_ids % EXP_DEV) == half
    slot_iota = jnp.arange(slots, dtype=jnp.int32)[:, None]
    picks = [
        (local_slot[:, k][None, :] == slot_iota) & owned[:, k][None, :]
        for k in range(route_ids.shape[1])
    ]
    dispatch = picks[0]
    for extra in picks[1:]:
        dispatch = dispatch | extra
    gate_slot = sum(
        jnp.sum(jnp.where(pick, gates[:, k][None, :], 0.0), axis=1) for k, pick in enumerate(picks)
    )
    dispatch_mat = dispatch.astype(bf16)

    x_buf = jnp.dot(dispatch_mat, sub_x, preferred_element_type=f32).astype(bf16)
    dy_buf = jnp.dot(dispatch_mat, sub_dy, preferred_element_type=f32)
    d_buf = (gate_slot[:, None] * dy_buf).astype(bf16)

    def to_experts(buf):
        got = lax.all_to_all(
            buf.reshape(sections, capacity, sub_w), "attn", split_axis=0, concat_axis=0, tiled=True
        ).reshape(slots, EXP_DEV, slice_w)
        by_shift = [got] + [lax.ppermute(got, "exp", core_shift(s)) for s in range(1, cores)]
        ordered = []
        for source in range(cores):
            picked = None
            for s, value in enumerate(by_shift):
                if picked is None:
                    picked = value
                else:
                    picked = jnp.where((core - s) % cores == source, value, picked)
            ordered.append(picked)
        return jnp.stack(ordered, axis=2).reshape(slots, model_width)

    x_rows = to_experts(x_buf)
    d_rows = to_experts(d_buf)

    if n_loc == 1:
        up_mat = w_up[0]
    else:
        up_mat = jnp.transpose(w_up, (1, 0, 2)).reshape(model_width, n_loc * hid_loc)
    down_mat = w_down.reshape(n_loc * hid_loc, model_width)

    pre_act = jnp.dot(x_rows, up_mat, preferred_element_type=f32)
    gelu_value, gelu_slope = gelu_parts(pre_act)
    activation = gelu_value.astype(bf16)
    grad_act = jnp.einsum("sd,hd->sh", d_rows, down_mat, preferred_element_type=f32)
    grad_pre = (grad_act * gelu_slope).astype(bf16)
    grad_down = jnp.einsum("sh,sd->hd", activation, d_rows, preferred_element_type=f32)
    grad_up = jnp.einsum("sd,sh->dh", x_rows, grad_pre, preferred_element_type=f32)

    out_loc = None
    dx_loc = None
    for g in range(n_loc):
        part = slice(g * hid_loc, (g + 1) * hid_loc)
        out_g = jnp.dot(activation[:, part], w_down[g], preferred_element_type=f32)
        dx_g = jnp.einsum("sh,dh->sd", grad_pre[:, part], w_up[g], preferred_element_type=f32)
        out_g = out_g.astype(bf16).astype(f32)
        dx_g = dx_g.astype(bf16).astype(f32)
        out_loc = out_g if out_loc is None else out_loc + out_g
        dx_loc = dx_g if dx_loc is None else dx_loc + dx_g

    def to_sections(rows):
        split = rows.reshape(slots, EXP_DEV, cores, slice_w)
        summed = lax.dynamic_index_in_dim(split, core, 2, keepdims=False)
        for s in range(1, cores):
            theirs = lax.dynamic_index_in_dim(split, (core + s) % cores, 2, keepdims=False)
            got = lax.ppermute(theirs.astype(bf16), "exp", core_shift(s))
            summed = summed + got.astype(f32)
        back = lax.all_to_all(
            summed.astype(bf16).reshape(sections, capacity, sub_w),
            "attn", split_axis=0, concat_axis=0, tiled=True,
        )
        return back.reshape(slots, sub_w)

    back_out = to_sections(out_loc)
    back_dx = to_sections(dx_loc)

    mixed_sub = None
    for k, pick in enumerate(picks):
        picked = jnp.dot(pick.astype(bf16).T, back_out, preferred_element_type=f32)
        term = gates[:, k][:, None] * picked
        mixed_sub = term if mixed_sub is None else mixed_sub + term
    dx_sub = jnp.dot(dispatch_mat.T, back_dx, preferred_element_type=f32)

    def finish(sub):
        split = sub.reshape(token_count, EXP_DEV, slice_w)
        keep = lax.dynamic_index_in_dim(split, half, 1, keepdims=False)
        give = lax.dynamic_index_in_dim(split, (half + 1) % EXP_DEV, 1, keepdims=False)
        return (keep + lax.ppermute(give, "exp", half_swap)).astype(bf16)

    mixed = finish(mixed_sub)
    grad_patches = finish(dx_sub)
    grad_up = jnp.transpose(grad_up.reshape(model_width, n_loc, hid_loc), (1, 0, 2))
    grad_down = grad_down.reshape(n_loc, hid_loc, model_width)
    return (mixed, grad_patches, grad_up, grad_down)


def solution(mesh):
    return jax.shard_map(
        on_device,
        mesh=mesh,
        in_specs=(
            P("attn", "exp"),
            P("attn", "exp"),
            P("attn", None),
            P("attn", None),
            P(("attn", "exp"), None, None),
            P(("attn", "exp"), None, None),
        ),
        out_specs=(
            P("attn", "exp"),
            P("attn", "exp"),
            P(("attn", "exp"), None, None),
            P(("attn", "exp"), None, None),
        ),
        check_vma=False,
    )
```

```python
import jax
import jax.numpy as jnp
from jax import lax
from jax.sharding import PartitionSpec as P

EXP_DEV = 2


def gelu_parts(pre_act):
    inner_arg = 0.7978845608 * (pre_act + 0.044715 * pre_act * pre_act * pre_act)
    tanh_val = jnp.tanh(inner_arg)
    gelu_value = 0.5 * pre_act * (1.0 + tanh_val)
    gelu_slope = 0.5 * (1.0 + tanh_val) + 0.5 * pre_act * (
        1.0 - tanh_val * tanh_val
    ) * 0.7978845608 * (1.0 + 0.134145 * pre_act * pre_act)
    return (gelu_value, gelu_slope)


def route_slots(route_ids, experts, capacity):
    flat_ids = route_ids.reshape(-1)
    one_hot = (flat_ids[:, None] == jnp.arange(experts, dtype=jnp.int32)[None, :]).astype(jnp.int32)
    before = jnp.cumsum(one_hot, axis=0) - one_hot
    rank_in = jnp.sum(before * one_hot, axis=1).reshape(route_ids.shape)
    return (route_ids // EXP_DEV) * capacity + rank_in


def on_device(patches, grad_out, route_ids, gates, w_up, w_down):
    sections = lax.axis_size("attn")
    n_exp = lax.axis_size("exp")
    cores = n_exp // EXP_DEV
    me = lax.axis_index("exp")
    half = me // cores
    core = me % cores
    experts = EXP_DEV * sections
    token_count, slice_w = patches.shape
    capacity = 4 * token_count // experts
    slots = sections * capacity
    n_loc, model_width, hid_loc = w_up.shape
    sub_w = EXP_DEV * slice_w
    f32 = jnp.float32
    bf16 = jnp.bfloat16

    def core_shift(s):
        return [(i, (i // cores) * cores + (i % cores + s) % cores) for i in range(n_exp)]

    half_swap = [(i, (i + cores) % n_exp) for i in range(n_exp)]

    def core_subset(local):
        other = lax.ppermute(local, "exp", half_swap)
        first = half == 0
        return jnp.concatenate(
            [jnp.where(first, local, other), jnp.where(first, other, local)], axis=1
        )

    sub_x = core_subset(patches)
    sub_dy = core_subset(grad_out)

    local_slot = route_slots(route_ids, experts, capacity)
    owned = (route_ids % EXP_DEV) == half
    slot_iota = jnp.arange(slots, dtype=jnp.int32)[:, None]
    picks = [
        (local_slot[:, k][None, :] == slot_iota) & owned[:, k][None, :]
        for k in range(route_ids.shape[1])
    ]
    dispatch = picks[0]
    for extra in picks[1:]:
        dispatch = dispatch | extra
    gate_slot = sum(
        jnp.sum(jnp.where(pick, gates[:, k][None, :], 0.0), axis=1) for k, pick in enumerate(picks)
    )
    dispatch_mat = dispatch.astype(bf16)

    x_buf = jnp.dot(dispatch_mat, sub_x, preferred_element_type=f32).astype(bf16)
    dy_buf = jnp.dot(dispatch_mat, sub_dy, preferred_element_type=f32)
    d_buf = (gate_slot[:, None] * dy_buf).astype(bf16)

    def pick_by(index, values):
        picked = values[0]
        for i, value in enumerate(values[1:], start=1):
            picked = jnp.where(index == i, value, picked)
        return picked

    def to_experts(buf):
        got = lax.all_to_all(
            buf.reshape(sections, capacity, sub_w), "attn", split_axis=0, concat_axis=0, tiled=True
        ).reshape(slots, sub_w)
        by_shift = [got] + [lax.ppermute(got, "exp", core_shift(s)) for s in range(1, cores)]
        ordered = [pick_by((core - source) % cores, by_shift) for source in range(cores)]
        return jnp.concatenate(
            [ordered[q][:, p * slice_w:(p + 1) * slice_w] for p in range(EXP_DEV) for q in range(cores)],
            axis=1,
        )

    x_rows = to_experts(x_buf)
    d_rows = to_experts(d_buf)

    if n_loc == 1:
        up_mat = w_up[0]
    else:
        up_mat = jnp.transpose(w_up, (1, 0, 2)).reshape(model_width, n_loc * hid_loc)
    down_mat = w_down.reshape(n_loc * hid_loc, model_width)

    pre_act = jnp.dot(x_rows, up_mat, preferred_element_type=f32)
    gelu_value, gelu_slope = gelu_parts(pre_act)
    activation = gelu_value.astype(bf16)
    grad_act = jnp.einsum("sd,hd->sh", d_rows, down_mat, preferred_element_type=f32)
    grad_pre = (grad_act * gelu_slope).astype(bf16)
    grad_down = jnp.einsum("sh,sd->hd", activation, d_rows, preferred_element_type=f32)
    grad_up = jnp.einsum("sd,sh->dh", x_rows, grad_pre, preferred_element_type=f32)

    out_loc = None
    dx_loc = None
    for g in range(n_loc):
        part = slice(g * hid_loc, (g + 1) * hid_loc)
        out_g = jnp.dot(activation[:, part], w_down[g], preferred_element_type=f32)
        dx_g = jnp.einsum("sh,dh->sd", grad_pre[:, part], w_up[g], preferred_element_type=f32)
        out_g = out_g.astype(bf16).astype(f32)
        dx_g = dx_g.astype(bf16).astype(f32)
        out_loc = out_g if out_loc is None else out_loc + out_g
        dx_loc = dx_g if dx_loc is None else dx_loc + dx_g

    def to_sections(rows):
        subsets = [
            jnp.concatenate(
                [rows[:, (p * cores + q) * slice_w:(p * cores + q + 1) * slice_w] for p in range(EXP_DEV)],
                axis=1,
            )
            for q in range(cores)
        ]
        summed = pick_by(core, subsets)
        for s in range(1, cores):
            theirs = pick_by((core + s) % cores, subsets)
            got = lax.ppermute(theirs.astype(bf16), "exp", core_shift(s))
            summed = summed + got.astype(f32)
        back = lax.all_to_all(
            summed.astype(bf16).reshape(sections, capacity, sub_w),
            "attn", split_axis=0, concat_axis=0, tiled=True,
        )
        return back.reshape(slots, sub_w)

    back_out = to_sections(out_loc)
    back_dx = to_sections(dx_loc)

    mixed_sub = None
    for k, pick in enumerate(picks):
        picked = jnp.dot(pick.astype(bf16).T, back_out, preferred_element_type=f32)
        term = gates[:, k][:, None] * picked
        mixed_sub = term if mixed_sub is None else mixed_sub + term
    dx_sub = jnp.dot(dispatch_mat.T, back_dx, preferred_element_type=f32)

    def finish(sub):
        pieces = [sub[:, p * slice_w:(p + 1) * slice_w] for p in range(EXP_DEV)]
        keep = pick_by(half, pieces)
        give = pick_by((half + 1) % EXP_DEV, pieces)
        return (keep + lax.ppermute(give, "exp", half_swap)).astype(bf16)

    mixed = finish(mixed_sub)
    grad_patches = finish(dx_sub)
    grad_up = jnp.transpose(grad_up.reshape(model_width, n_loc, hid_loc), (1, 0, 2))
    grad_down = grad_down.reshape(n_loc, hid_loc, model_width)
    return (mixed, grad_patches, grad_up, grad_down)


def solution(mesh):
    return jax.shard_map(
        on_device,
        mesh=mesh,
        in_specs=(
            P("attn", "exp"),
            P("attn", "exp"),
            P("attn", None),
            P("attn", None),
            P(("attn", "exp"), None, None),
            P(("attn", "exp"), None, None),
        ),
        out_specs=(
            P("attn", "exp"),
            P("attn", "exp"),
            P(("attn", "exp"), None, None),
            P(("attn", "exp"), None, None),
        ),
        check_vma=False,
    )
```

```python
import jax
import jax.numpy as jnp
from jax import lax
from jax.sharding import PartitionSpec as P

EXP_DEV = 2


def gelu_parts(pre_act):
    inner_arg = 0.7978845608 * (pre_act + 0.044715 * pre_act * pre_act * pre_act)
    tanh_val = jnp.tanh(inner_arg)
    gelu_value = 0.5 * pre_act * (1.0 + tanh_val)
    gelu_slope = 0.5 * (1.0 + tanh_val) + 0.5 * pre_act * (
        1.0 - tanh_val * tanh_val
    ) * 0.7978845608 * (1.0 + 0.134145 * pre_act * pre_act)
    return (gelu_value, gelu_slope)


def route_slots(route_ids, experts, capacity):
    flat_ids = route_ids.reshape(-1)
    one_hot = (flat_ids[:, None] == jnp.arange(experts, dtype=jnp.int32)[None, :]).astype(jnp.int32)
    before = jnp.cumsum(one_hot, axis=0) - one_hot
    rank_in = jnp.sum(before * one_hot, axis=1).reshape(route_ids.shape)
    return (route_ids // EXP_DEV) * capacity + rank_in


def on_device(patches, grad_out, route_ids, gates, w_up, w_down):
    sections = lax.axis_size("attn")
    n_exp = lax.axis_size("exp")
    cores = n_exp // EXP_DEV
    me = lax.axis_index("exp")
    half = me // cores
    core = me % cores
    experts = EXP_DEV * sections
    token_count, slice_w = patches.shape
    capacity = 4 * token_count // experts
    slots = sections * capacity
    n_loc, model_width, hid_loc = w_up.shape
    sub_w = EXP_DEV * slice_w
    f32 = jnp.float32
    bf16 = jnp.bfloat16

    def core_shift(s):
        return [(i, (i // cores) * cores + (i % cores + s) % cores) for i in range(n_exp)]

    half_swap = [(i, (i + cores) % n_exp) for i in range(n_exp)]

    def core_subset(local):
        other = lax.ppermute(local, "exp", half_swap)
        first = half == 0
        return jnp.concatenate(
            [jnp.where(first, local, other), jnp.where(first, other, local)], axis=1
        )

    sub_x = core_subset(patches)

    local_slot = route_slots(route_ids, experts, capacity)
    owned = (route_ids % EXP_DEV) == half
    slot_iota = jnp.arange(slots, dtype=jnp.int32)[:, None]
    picks = [
        (local_slot[:, k][None, :] == slot_iota) & owned[:, k][None, :]
        for k in range(route_ids.shape[1])
    ]
    dispatch = picks[0]
    for extra in picks[1:]:
        dispatch = dispatch | extra
    gate_slot = sum(
        jnp.sum(jnp.where(pick, gates[:, k][None, :], 0.0), axis=1) for k, pick in enumerate(picks)
    )
    dispatch_mat = dispatch.astype(bf16)

    x_buf = jnp.dot(dispatch_mat, sub_x, preferred_element_type=f32).astype(bf16)
    grad_out, x_buf = lax.optimization_barrier((grad_out, x_buf))
    sub_dy = core_subset(grad_out)
    dy_buf = jnp.dot(dispatch_mat, sub_dy, preferred_element_type=f32)
    d_buf = (gate_slot[:, None] * dy_buf).astype(bf16)

    def pick_by(index, values):
        picked = values[0]
        for i, value in enumerate(values[1:], start=1):
            picked = jnp.where(index == i, value, picked)
        return picked

    def to_experts(buf):
        got = lax.all_to_all(
            buf.reshape(sections, capacity, sub_w), "attn", split_axis=0, concat_axis=0, tiled=True
        ).reshape(slots, sub_w)
        by_shift = [got] + [lax.ppermute(got, "exp", core_shift(s)) for s in range(1, cores)]
        ordered = [pick_by((core - source) % cores, by_shift) for source in range(cores)]
        return jnp.concatenate(
            [ordered[q][:, p * slice_w:(p + 1) * slice_w] for p in range(EXP_DEV) for q in range(cores)],
            axis=1,
        )

    x_rows = to_experts(x_buf)
    d_buf, x_rows = lax.optimization_barrier((d_buf, x_rows))
    d_rows = to_experts(d_buf)

    if n_loc == 1:
        up_mat = w_up[0]
    else:
        up_mat = jnp.transpose(w_up, (1, 0, 2)).reshape(model_width, n_loc * hid_loc)
    down_mat = w_down.reshape(n_loc * hid_loc, model_width)

    pre_act = jnp.dot(x_rows, up_mat, preferred_element_type=f32)
    gelu_value, gelu_slope = gelu_parts(pre_act)
    activation = gelu_value.astype(bf16)
    grad_act = jnp.einsum("sd,hd->sh", d_rows, down_mat, preferred_element_type=f32)
    grad_pre = (grad_act * gelu_slope).astype(bf16)

    out_loc = None
    dx_loc = None
    for g in range(n_loc):
        part = slice(g * hid_loc, (g + 1) * hid_loc)
        out_g = jnp.dot(activation[:, part], w_down[g], preferred_element_type=f32)
        dx_g = jnp.einsum("sh,dh->sd", grad_pre[:, part], w_up[g], preferred_element_type=f32)
        out_g = out_g.astype(bf16).astype(f32)
        dx_g = dx_g.astype(bf16).astype(f32)
        out_loc = out_g if out_loc is None else out_loc + out_g
        dx_loc = dx_g if dx_loc is None else dx_loc + dx_g

    def to_sections(rows, hold):
        subsets = [
            jnp.concatenate(
                [rows[:, (p * cores + q) * slice_w:(p * cores + q + 1) * slice_w] for p in range(EXP_DEV)],
                axis=1,
            )
            for q in range(cores)
        ]
        summed = pick_by(core, subsets)
        for s in range(1, cores):
            theirs = pick_by((core + s) % cores, subsets)
            got = lax.ppermute(theirs.astype(bf16), "exp", core_shift(s))
            summed = summed + got.astype(f32)
        sent, hold = lax.optimization_barrier((summed.astype(bf16), hold))
        back = lax.all_to_all(
            sent.reshape(sections, capacity, sub_w), "attn", split_axis=0, concat_axis=0, tiled=True
        )
        return back.reshape(slots, sub_w), hold

    back_out, (act_late, d_late) = to_sections(out_loc, (activation, d_rows))
    grad_down = jnp.einsum("sh,sd->hd", act_late, d_late, preferred_element_type=f32)
    back_dx, (x_late, pre_late) = to_sections(dx_loc, (x_rows, grad_pre))
    grad_up = jnp.einsum("sd,sh->dh", x_late, pre_late, preferred_element_type=f32)

    mixed_sub = None
    for k, pick in enumerate(picks):
        picked = jnp.dot(pick.astype(bf16).T, back_out, preferred_element_type=f32)
        term = gates[:, k][:, None] * picked
        mixed_sub = term if mixed_sub is None else mixed_sub + term
    dx_sub = jnp.dot(dispatch_mat.T, back_dx, preferred_element_type=f32)

    def finish(sub):
        pieces = [sub[:, p * slice_w:(p + 1) * slice_w] for p in range(EXP_DEV)]
        keep = pick_by(half, pieces)
        give = pick_by((half + 1) % EXP_DEV, pieces)
        return (keep + lax.ppermute(give, "exp", half_swap)).astype(bf16)

    mixed = finish(mixed_sub)
    grad_patches = finish(dx_sub)
    grad_up = jnp.transpose(grad_up.reshape(model_width, n_loc, hid_loc), (1, 0, 2))
    grad_down = grad_down.reshape(n_loc, hid_loc, model_width)
    return (mixed, grad_patches, grad_up, grad_down)


def solution(mesh):
    return jax.shard_map(
        on_device,
        mesh=mesh,
        in_specs=(
            P("attn", "exp"),
            P("attn", "exp"),
            P("attn", None),
            P("attn", None),
            P(("attn", "exp"), None, None),
            P(("attn", "exp"), None, None),
        ),
        out_specs=(
            P("attn", "exp"),
            P("attn", "exp"),
            P(("attn", "exp"), None, None),
            P(("attn", "exp"), None, None),
        ),
        check_vma=False,
    )
```

```python
import jax
import jax.numpy as jnp
from jax import lax
from jax.sharding import PartitionSpec as P

EXP_DEV = 2


def gelu_parts(pre_act):
    inner_arg = 0.7978845608 * (pre_act + 0.044715 * pre_act * pre_act * pre_act)
    tanh_val = jnp.tanh(inner_arg)
    gelu_value = 0.5 * pre_act * (1.0 + tanh_val)
    gelu_slope = 0.5 * (1.0 + tanh_val) + 0.5 * pre_act * (
        1.0 - tanh_val * tanh_val
    ) * 0.7978845608 * (1.0 + 0.134145 * pre_act * pre_act)
    return (gelu_value, gelu_slope)


def route_slots(route_ids, experts, capacity):
    flat_ids = route_ids.reshape(-1)
    one_hot = (flat_ids[:, None] == jnp.arange(experts, dtype=jnp.int32)[None, :]).astype(jnp.int32)
    before = jnp.cumsum(one_hot, axis=0) - one_hot
    rank_in = jnp.sum(before * one_hot, axis=1).reshape(route_ids.shape)
    return (route_ids // EXP_DEV) * capacity + rank_in


def on_device(patches, grad_out, route_ids, gates, w_up, w_down):
    sections = lax.axis_size("attn")
    n_exp = lax.axis_size("exp")
    cores = n_exp // EXP_DEV
    me = lax.axis_index("exp")
    half = me // cores
    core = me % cores
    experts = EXP_DEV * sections
    token_count, slice_w = patches.shape
    capacity = 4 * token_count // experts
    slots = sections * capacity
    n_loc, model_width, hid_loc = w_up.shape
    sub_w = EXP_DEV * slice_w
    f32 = jnp.float32
    bf16 = jnp.bfloat16

    def core_shift(s):
        return [(i, (i // cores) * cores + (i % cores + s) % cores) for i in range(n_exp)]

    half_swap = [(i, (i + cores) % n_exp) for i in range(n_exp)]

    def core_subset(local):
        other = lax.ppermute(local, "exp", half_swap)
        first = half == 0
        return jnp.concatenate(
            [jnp.where(first, local, other), jnp.where(first, other, local)], axis=1
        )

    sub_x = core_subset(patches)

    local_slot = route_slots(route_ids, experts, capacity)
    owned = (route_ids % EXP_DEV) == half
    slot_iota = jnp.arange(slots, dtype=jnp.int32)[:, None]
    picks = [
        (local_slot[:, k][None, :] == slot_iota) & owned[:, k][None, :]
        for k in range(route_ids.shape[1])
    ]
    dispatch = picks[0]
    for extra in picks[1:]:
        dispatch = dispatch | extra
    gate_slot = sum(
        jnp.sum(jnp.where(pick, gates[:, k][None, :], 0.0), axis=1) for k, pick in enumerate(picks)
    )
    dispatch_mat = dispatch.astype(bf16)

    x_buf = jnp.dot(dispatch_mat, sub_x, preferred_element_type=f32).astype(bf16)
    grad_out, x_buf = lax.optimization_barrier((grad_out, x_buf))
    sub_dy = core_subset(grad_out)
    dy_buf = jnp.dot(dispatch_mat, sub_dy, preferred_element_type=f32)
    d_buf = (gate_slot[:, None] * dy_buf).astype(bf16)

    def pick_by(index, values):
        picked = values[0]
        for i, value in enumerate(values[1:], start=1):
            picked = jnp.where(index == i, value, picked)
        return picked

    def to_experts(buf):
        got = lax.all_to_all(
            buf.reshape(sections, capacity, sub_w), "attn", split_axis=0, concat_axis=0, tiled=True
        ).reshape(slots, sub_w)
        by_shift = [got] + [lax.ppermute(got, "exp", core_shift(s)) for s in range(1, cores)]
        ordered = [pick_by((core - source) % cores, by_shift) for source in range(cores)]
        return jnp.concatenate(
            [ordered[q][:, p * slice_w:(p + 1) * slice_w] for p in range(EXP_DEV) for q in range(cores)],
            axis=1,
        )

    x_rows = to_experts(x_buf)
    d_buf, x_rows = lax.optimization_barrier((d_buf, x_rows))
    d_rows = to_experts(d_buf)

    if n_loc == 1:
        up_mat = w_up[0]
    else:
        up_mat = jnp.transpose(w_up, (1, 0, 2)).reshape(model_width, n_loc * hid_loc)
    down_mat = w_down.reshape(n_loc * hid_loc, model_width)

    pre_act = jnp.dot(x_rows, up_mat, preferred_element_type=f32)
    gelu_value, gelu_slope = gelu_parts(pre_act)
    activation = gelu_value.astype(bf16)
    grad_act = jnp.einsum("sd,hd->sh", d_rows, down_mat, preferred_element_type=f32)
    grad_pre = (grad_act * gelu_slope).astype(bf16)

    out_loc = None
    dx_loc = None
    for g in range(n_loc):
        part = slice(g * hid_loc, (g + 1) * hid_loc)
        out_g = jnp.dot(activation[:, part], w_down[g], preferred_element_type=f32)
        dx_g = jnp.einsum("sh,dh->sd", grad_pre[:, part], w_up[g], preferred_element_type=f32)
        out_g = out_g.astype(bf16).astype(f32)
        dx_g = dx_g.astype(bf16).astype(f32)
        out_loc = out_g if out_loc is None else out_loc + out_g
        dx_loc = dx_g if dx_loc is None else dx_loc + dx_g

    def to_sections(rows, hold):
        subsets = [
            jnp.concatenate(
                [rows[:, (p * cores + q) * slice_w:(p * cores + q + 1) * slice_w] for p in range(EXP_DEV)],
                axis=1,
            )
            for q in range(cores)
        ]
        summed = pick_by(core, subsets)
        for s in range(1, cores):
            theirs = pick_by((core + s) % cores, subsets)
            got = lax.ppermute(theirs.astype(bf16), "exp", core_shift(s))
            summed = summed + got.astype(f32)
        sent, hold = lax.optimization_barrier((summed.astype(bf16), hold))
        back = lax.all_to_all(
            sent.reshape(sections, capacity, sub_w), "attn", split_axis=0, concat_axis=0, tiled=True
        )
        return back.reshape(slots, sub_w), hold

    back_out, (act_late, d_late) = to_sections(out_loc, (activation, d_rows))
    grad_down = jnp.einsum("sh,sd->hd", act_late, d_late, preferred_element_type=f32)
    back_dx, (x_late, pre_late, grad_down) = to_sections(dx_loc, (x_rows, grad_pre, grad_down))
    grad_up = jnp.einsum("sd,sh->dh", x_late, pre_late, preferred_element_type=f32)
    back_dx, grad_up = lax.optimization_barrier((back_dx, grad_up))

    mixed_sub = None
    for k, pick in enumerate(picks):
        picked = jnp.dot(pick.astype(bf16).T, back_out, preferred_element_type=f32)
        term = gates[:, k][:, None] * picked
        mixed_sub = term if mixed_sub is None else mixed_sub + term
    dx_sub = jnp.dot(dispatch_mat.T, back_dx, preferred_element_type=f32)

    def finish(sub):
        pieces = [sub[:, p * slice_w:(p + 1) * slice_w] for p in range(EXP_DEV)]
        keep = pick_by(half, pieces)
        give = pick_by((half + 1) % EXP_DEV, pieces)
        return (keep + lax.ppermute(give, "exp", half_swap)).astype(bf16)

    mixed = finish(mixed_sub)
    grad_patches = finish(dx_sub)
    grad_up = jnp.transpose(grad_up.reshape(model_width, n_loc, hid_loc), (1, 0, 2))
    grad_down = grad_down.reshape(n_loc, hid_loc, model_width)
    return (mixed, grad_patches, grad_up, grad_down)


def solution(mesh):
    return jax.shard_map(
        on_device,
        mesh=mesh,
        in_specs=(
            P("attn", "exp"),
            P("attn", "exp"),
            P("attn", None),
            P("attn", None),
            P(("attn", "exp"), None, None),
            P(("attn", "exp"), None, None),
        ),
        out_specs=(
            P("attn", "exp"),
            P("attn", "exp"),
            P(("attn", "exp"), None, None),
            P(("attn", "exp"), None, None),
        ),
        check_vma=False,
    )
```

```python
import jax
import jax.numpy as jnp
from jax import lax
from jax.sharding import PartitionSpec as P

EXP_DEV = 2


def gelu_parts(pre_act):
    inner_arg = 0.7978845608 * (pre_act + 0.044715 * pre_act * pre_act * pre_act)
    tanh_val = jnp.tanh(inner_arg)
    gelu_value = 0.5 * pre_act * (1.0 + tanh_val)
    gelu_slope = 0.5 * (1.0 + tanh_val) + 0.5 * pre_act * (
        1.0 - tanh_val * tanh_val
    ) * 0.7978845608 * (1.0 + 0.134145 * pre_act * pre_act)
    return (gelu_value, gelu_slope)


def route_slots(route_ids, experts, capacity):
    flat_ids = route_ids.reshape(-1)
    one_hot = (flat_ids[:, None] == jnp.arange(experts, dtype=jnp.int32)[None, :]).astype(jnp.int32)
    before = jnp.cumsum(one_hot, axis=0) - one_hot
    rank_in = jnp.sum(before * one_hot, axis=1).reshape(route_ids.shape)
    return (route_ids // EXP_DEV) * capacity + rank_in


def on_device(patches, grad_out, route_ids, gates, w_up, w_down):
    sections = lax.axis_size("attn")
    n_exp = lax.axis_size("exp")
    cores = n_exp // EXP_DEV
    me = lax.axis_index("exp")
    half = me // cores
    core = me % cores
    experts = EXP_DEV * sections
    token_count, slice_w = patches.shape
    capacity = 4 * token_count // experts
    slots = sections * capacity
    n_loc, model_width, hid_loc = w_up.shape
    sub_w = EXP_DEV * slice_w
    f32 = jnp.float32
    bf16 = jnp.bfloat16

    def core_shift(s):
        return [(i, (i // cores) * cores + (i % cores + s) % cores) for i in range(n_exp)]

    half_swap = [(i, (i + cores) % n_exp) for i in range(n_exp)]

    def core_subset(local):
        other = lax.ppermute(local, "exp", half_swap)
        first = half == 0
        return jnp.concatenate(
            [jnp.where(first, local, other), jnp.where(first, other, local)], axis=1
        )

    def pick_by(index, values):
        picked = values[0]
        for i, value in enumerate(values[1:], start=1):
            picked = jnp.where(index == i, value, picked)
        return picked

    def to_experts(got):
        by_shift = [got] + [lax.ppermute(got, "exp", core_shift(s)) for s in range(1, cores)]
        ordered = [pick_by((core - source) % cores, by_shift) for source in range(cores)]
        return jnp.concatenate(
            [ordered[q][:, p * slice_w:(p + 1) * slice_w] for p in range(EXP_DEV) for q in range(cores)],
            axis=1,
        )

    local_slot = route_slots(route_ids, experts, capacity)
    owned = (route_ids % EXP_DEV) == half
    slot_iota = jnp.arange(slots, dtype=jnp.int32)[:, None]
    picks = [
        (local_slot[:, k][None, :] == slot_iota) & owned[:, k][None, :]
        for k in range(route_ids.shape[1])
    ]
    dispatch = picks[0]
    for extra in picks[1:]:
        dispatch = dispatch | extra
    gate_slot = sum(
        jnp.sum(jnp.where(pick, gates[:, k][None, :], 0.0), axis=1) for k, pick in enumerate(picks)
    )
    dispatch_mat = dispatch.astype(bf16)

    def send(buf):
        width = buf.shape[-1]
        return lax.all_to_all(
            buf.reshape(sections, capacity, width), "attn", split_axis=0, concat_axis=0, tiled=True
        ).reshape(slots, width)

    got_own = send(jnp.dot(dispatch_mat, patches, preferred_element_type=f32).astype(bf16))
    x_other = lax.ppermute(patches, "exp", half_swap)
    got_other = send(jnp.dot(dispatch_mat, x_other, preferred_element_type=f32).astype(bf16))
    first = half == 0
    got_x = jnp.concatenate(
        [jnp.where(first, got_own, got_other), jnp.where(first, got_other, got_own)], axis=1
    )
    grad_out, got_x = lax.optimization_barrier((grad_out, got_x))
    sub_dy = core_subset(grad_out)
    dy_buf = jnp.dot(dispatch_mat, sub_dy, preferred_element_type=f32)
    d_buf = (gate_slot[:, None] * dy_buf).astype(bf16)
    x_rows = to_experts(got_x)
    d_buf, x_rows = lax.optimization_barrier((d_buf, x_rows))
    d_rows = to_experts(send(d_buf))

    if n_loc == 1:
        up_mat = w_up[0]
    else:
        up_mat = jnp.transpose(w_up, (1, 0, 2)).reshape(model_width, n_loc * hid_loc)
    down_mat = w_down.reshape(n_loc * hid_loc, model_width)

    pre_act = jnp.dot(x_rows, up_mat, preferred_element_type=f32)
    gelu_value, gelu_slope = gelu_parts(pre_act)
    activation = gelu_value.astype(bf16)
    grad_act = jnp.einsum("sd,hd->sh", d_rows, down_mat, preferred_element_type=f32)
    grad_pre = (grad_act * gelu_slope).astype(bf16)

    out_loc = None
    dx_loc = None
    for g in range(n_loc):
        part = slice(g * hid_loc, (g + 1) * hid_loc)
        out_g = jnp.dot(activation[:, part], w_down[g], preferred_element_type=f32)
        dx_g = jnp.einsum("sh,dh->sd", grad_pre[:, part], w_up[g], preferred_element_type=f32)
        out_g = out_g.astype(bf16).astype(f32)
        dx_g = dx_g.astype(bf16).astype(f32)
        out_loc = out_g if out_loc is None else out_loc + out_g
        dx_loc = dx_g if dx_loc is None else dx_loc + dx_g

    def group_sum(rows, hold):
        subsets = [
            jnp.concatenate(
                [rows[:, (p * cores + q) * slice_w:(p * cores + q + 1) * slice_w] for p in range(EXP_DEV)],
                axis=1,
            )
            for q in range(cores)
        ]
        summed = pick_by(core, subsets)
        for s in range(1, cores):
            theirs = pick_by((core + s) % cores, subsets)
            got = lax.ppermute(theirs.astype(bf16), "exp", core_shift(s))
            summed = summed + got.astype(f32)
        return lax.optimization_barrier((summed.astype(bf16), hold))

    def finish(sub):
        pieces = [sub[:, p * slice_w:(p + 1) * slice_w] for p in range(EXP_DEV)]
        keep = pick_by(half, pieces)
        give = pick_by((half + 1) % EXP_DEV, pieces)
        return (keep + lax.ppermute(give, "exp", half_swap)).astype(bf16)

    sum_out, (act_late, d_late) = group_sum(out_loc, (activation, d_rows))
    back_out = send(sum_out)
    grad_down = jnp.einsum("sh,sd->hd", act_late, d_late, preferred_element_type=f32)
    sum_dx, (x_late, pre_late, grad_down) = group_sum(dx_loc, (x_rows, grad_pre, grad_down))
    dx_pieces = [sum_dx[:, p * slice_w:(p + 1) * slice_w] for p in range(EXP_DEV)]
    back_give = send(pick_by((half + 1) % EXP_DEV, dx_pieces))
    grad_up = jnp.einsum("sd,sh->dh", x_late, pre_late, preferred_element_type=f32)
    back_give, grad_up = lax.optimization_barrier((back_give, grad_up))
    dx_give = jnp.dot(dispatch_mat.T, back_give, preferred_element_type=f32)
    dx_came = lax.ppermute(dx_give, "exp", half_swap)
    back_keep = send(pick_by(half, dx_pieces))
    grad_patches = (jnp.dot(dispatch_mat.T, back_keep, preferred_element_type=f32) + dx_came).astype(bf16)

    mixed_sub = None
    for k, pick in enumerate(picks):
        picked = jnp.dot(pick.astype(bf16).T, back_out, preferred_element_type=f32)
        term = gates[:, k][:, None] * picked
        mixed_sub = term if mixed_sub is None else mixed_sub + term
    mixed = finish(mixed_sub)
    grad_up = jnp.transpose(grad_up.reshape(model_width, n_loc, hid_loc), (1, 0, 2))
    grad_down = grad_down.reshape(n_loc, hid_loc, model_width)
    return (mixed, grad_patches, grad_up, grad_down)


def solution(mesh):
    return jax.shard_map(
        on_device,
        mesh=mesh,
        in_specs=(
            P("attn", "exp"),
            P("attn", "exp"),
            P("attn", None),
            P("attn", None),
            P(("attn", "exp"), None, None),
            P(("attn", "exp"), None, None),
        ),
        out_specs=(
            P("attn", "exp"),
            P("attn", "exp"),
            P(("attn", "exp"), None, None),
            P(("attn", "exp"), None, None),
        ),
        check_vma=False,
    )
```

```python
import jax
import jax.numpy as jnp
from jax import lax
from jax.sharding import PartitionSpec as P

EXP_DEV = 2


def gelu_parts(pre_act):
    inner_arg = 0.7978845608 * (pre_act + 0.044715 * pre_act * pre_act * pre_act)
    tanh_val = jnp.tanh(inner_arg)
    gelu_value = 0.5 * pre_act * (1.0 + tanh_val)
    gelu_slope = 0.5 * (1.0 + tanh_val) + 0.5 * pre_act * (
        1.0 - tanh_val * tanh_val
    ) * 0.7978845608 * (1.0 + 0.134145 * pre_act * pre_act)
    return (gelu_value, gelu_slope)


def route_slots(route_ids, experts, capacity):
    flat_ids = route_ids.reshape(-1)
    one_hot = (flat_ids[:, None] == jnp.arange(experts, dtype=jnp.int32)[None, :]).astype(jnp.int32)
    before = jnp.cumsum(one_hot, axis=0) - one_hot
    rank_in = jnp.sum(before * one_hot, axis=1).reshape(route_ids.shape)
    return (route_ids // EXP_DEV) * capacity + rank_in


def on_device(patches, grad_out, route_ids, gates, w_up, w_down):
    sections = lax.axis_size("attn")
    n_exp = lax.axis_size("exp")
    cores = n_exp // EXP_DEV
    me = lax.axis_index("exp")
    half = me // cores
    core = me % cores
    experts = EXP_DEV * sections
    token_count, slice_w = patches.shape
    capacity = 4 * token_count // experts
    slots = sections * capacity
    n_loc, model_width, hid_loc = w_up.shape
    sub_w = EXP_DEV * slice_w
    f32 = jnp.float32
    bf16 = jnp.bfloat16

    def core_shift(s):
        return [(i, (i // cores) * cores + (i % cores + s) % cores) for i in range(n_exp)]

    half_swap = [(i, (i + cores) % n_exp) for i in range(n_exp)]

    def core_subset(local):
        other = lax.ppermute(local, "exp", half_swap)
        first = half == 0
        return jnp.concatenate(
            [jnp.where(first, local, other), jnp.where(first, other, local)], axis=1
        )

    def pick_by(index, values):
        picked = values[0]
        for i, value in enumerate(values[1:], start=1):
            picked = jnp.where(index == i, value, picked)
        return picked

    def to_experts(got):
        by_shift = [got] + [lax.ppermute(got, "exp", core_shift(s)) for s in range(1, cores)]
        ordered = [pick_by((core - source) % cores, by_shift) for source in range(cores)]
        return jnp.concatenate(
            [ordered[q][:, p * slice_w:(p + 1) * slice_w] for p in range(EXP_DEV) for q in range(cores)],
            axis=1,
        )

    local_slot = route_slots(route_ids, experts, capacity)
    owned = (route_ids % EXP_DEV) == half
    slot_iota = jnp.arange(slots, dtype=jnp.int32)[:, None]
    picks = [
        (local_slot[:, k][None, :] == slot_iota) & owned[:, k][None, :]
        for k in range(route_ids.shape[1])
    ]
    dispatch = picks[0]
    for extra in picks[1:]:
        dispatch = dispatch | extra
    gate_slot = sum(
        jnp.sum(jnp.where(pick, gates[:, k][None, :], 0.0), axis=1) for k, pick in enumerate(picks)
    )
    dispatch_mat = dispatch.astype(bf16)

    def send(buf):
        width = buf.shape[-1]
        return lax.all_to_all(
            buf.reshape(sections, capacity, width), "attn", split_axis=0, concat_axis=0, tiled=True
        ).reshape(slots, width)

    got_own = send(jnp.dot(dispatch_mat, patches, preferred_element_type=f32).astype(bf16))
    x_other = lax.ppermute(patches, "exp", half_swap)
    other_buf = jnp.dot(dispatch_mat, x_other, preferred_element_type=f32).astype(bf16)
    sub_dy = core_subset(grad_out)
    sub_dy, other_buf = lax.optimization_barrier((sub_dy, other_buf))
    got_other = send(other_buf)
    first = half == 0
    got_x = jnp.concatenate(
        [jnp.where(first, got_own, got_other), jnp.where(first, got_other, got_own)], axis=1
    )
    dy_buf = jnp.dot(dispatch_mat, sub_dy, preferred_element_type=f32)
    d_buf = (gate_slot[:, None] * dy_buf).astype(bf16)
    x_rows = to_experts(got_x)
    d_buf, x_rows = lax.optimization_barrier((d_buf, x_rows))
    got_d = send(d_buf)

    if n_loc == 1:
        up_mat = w_up[0]
    else:
        up_mat = jnp.transpose(w_up, (1, 0, 2)).reshape(model_width, n_loc * hid_loc)
    down_mat = w_down.reshape(n_loc * hid_loc, model_width)

    pre_act = jnp.dot(x_rows, up_mat, preferred_element_type=f32)
    gelu_value, gelu_slope = gelu_parts(pre_act)
    activation = gelu_value.astype(bf16)

    out_loc = None
    for g in range(n_loc):
        part = slice(g * hid_loc, (g + 1) * hid_loc)
        out_g = jnp.dot(activation[:, part], w_down[g], preferred_element_type=f32)
        out_g = out_g.astype(bf16).astype(f32)
        out_loc = out_g if out_loc is None else out_loc + out_g

    def group_sum(rows, hold):
        subsets = [
            jnp.concatenate(
                [rows[:, (p * cores + q) * slice_w:(p * cores + q + 1) * slice_w] for p in range(EXP_DEV)],
                axis=1,
            )
            for q in range(cores)
        ]
        summed = pick_by(core, subsets)
        for s in range(1, cores):
            theirs = pick_by((core + s) % cores, subsets)
            got = lax.ppermute(theirs.astype(bf16), "exp", core_shift(s))
            summed = summed + got.astype(f32)
        return lax.optimization_barrier((summed.astype(bf16), hold))

    def finish(sub):
        pieces = [sub[:, p * slice_w:(p + 1) * slice_w] for p in range(EXP_DEV)]
        keep = pick_by(half, pieces)
        give = pick_by((half + 1) % EXP_DEV, pieces)
        return (keep + lax.ppermute(give, "exp", half_swap)).astype(bf16)

    sum_out, got_d = group_sum(out_loc, got_d)
    back_out = send(sum_out)
    d_rows = to_experts(got_d)
    grad_act = jnp.einsum("sd,hd->sh", d_rows, down_mat, preferred_element_type=f32)
    grad_pre = (grad_act * gelu_slope).astype(bf16)
    dx_loc = None
    for g in range(n_loc):
        part = slice(g * hid_loc, (g + 1) * hid_loc)
        dx_g = jnp.einsum("sh,dh->sd", grad_pre[:, part], w_up[g], preferred_element_type=f32)
        dx_g = dx_g.astype(bf16).astype(f32)
        dx_loc = dx_g if dx_loc is None else dx_loc + dx_g
    grad_down = jnp.einsum("sh,sd->hd", activation, d_rows, preferred_element_type=f32)
    sum_dx, (x_late, pre_late, grad_down) = group_sum(dx_loc, (x_rows, grad_pre, grad_down))
    dx_pieces = [sum_dx[:, p * slice_w:(p + 1) * slice_w] for p in range(EXP_DEV)]
    back_give = send(pick_by((half + 1) % EXP_DEV, dx_pieces))
    grad_up = jnp.einsum("sd,sh->dh", x_late, pre_late, preferred_element_type=f32)
    back_give, grad_up = lax.optimization_barrier((back_give, grad_up))
    dx_give = jnp.dot(dispatch_mat.T, back_give, preferred_element_type=f32)
    dx_came = lax.ppermute(dx_give, "exp", half_swap)
    back_keep = send(pick_by(half, dx_pieces))
    grad_patches = (jnp.dot(dispatch_mat.T, back_keep, preferred_element_type=f32) + dx_came).astype(bf16)

    mixed_sub = None
    for k, pick in enumerate(picks):
        picked = jnp.dot(pick.astype(bf16).T, back_out, preferred_element_type=f32)
        term = gates[:, k][:, None] * picked
        mixed_sub = term if mixed_sub is None else mixed_sub + term
    mixed = finish(mixed_sub)
    grad_up = jnp.transpose(grad_up.reshape(model_width, n_loc, hid_loc), (1, 0, 2))
    grad_down = grad_down.reshape(n_loc, hid_loc, model_width)
    return (mixed, grad_patches, grad_up, grad_down)


def solution(mesh):
    return jax.shard_map(
        on_device,
        mesh=mesh,
        in_specs=(
            P("attn", "exp"),
            P("attn", "exp"),
            P("attn", None),
            P("attn", None),
            P(("attn", "exp"), None, None),
            P(("attn", "exp"), None, None),
        ),
        out_specs=(
            P("attn", "exp"),
            P("attn", "exp"),
            P(("attn", "exp"), None, None),
            P(("attn", "exp"), None, None),
        ),
        check_vma=False,
    )
```

```python
import jax
import jax.numpy as jnp
from jax import lax
from jax.sharding import PartitionSpec as P

EXP_DEV = 2


def gelu_parts(pre_act):
    inner_arg = 0.7978845608 * (pre_act + 0.044715 * pre_act * pre_act * pre_act)
    tanh_val = jnp.tanh(inner_arg)
    gelu_value = 0.5 * pre_act * (1.0 + tanh_val)
    gelu_slope = 0.5 * (1.0 + tanh_val) + 0.5 * pre_act * (
        1.0 - tanh_val * tanh_val
    ) * 0.7978845608 * (1.0 + 0.134145 * pre_act * pre_act)
    return (gelu_value, gelu_slope)


def route_slots(route_ids, experts, capacity):
    flat_ids = route_ids.reshape(-1)
    one_hot = (flat_ids[:, None] == jnp.arange(experts, dtype=jnp.int32)[None, :]).astype(jnp.int32)
    before = jnp.cumsum(one_hot, axis=0) - one_hot
    rank_in = jnp.sum(before * one_hot, axis=1).reshape(route_ids.shape)
    return (route_ids // EXP_DEV) * capacity + rank_in


def on_device(patches, grad_out, route_ids, gates, w_up, w_down):
    sections = lax.axis_size("attn")
    n_exp = lax.axis_size("exp")
    cores = n_exp // EXP_DEV
    me = lax.axis_index("exp")
    half = me // cores
    core = me % cores
    experts = EXP_DEV * sections
    token_count, slice_w = patches.shape
    capacity = 4 * token_count // experts
    slots = sections * capacity
    n_loc, model_width, hid_loc = w_up.shape
    sub_w = EXP_DEV * slice_w
    f32 = jnp.float32
    bf16 = jnp.bfloat16

    def core_shift(s):
        return [(i, (i // cores) * cores + (i % cores + s) % cores) for i in range(n_exp)]

    half_swap = [(i, (i + cores) % n_exp) for i in range(n_exp)]

    def core_subset(local):
        other = lax.ppermute(local, "exp", half_swap)
        first = half == 0
        return jnp.concatenate(
            [jnp.where(first, local, other), jnp.where(first, other, local)], axis=1
        )

    def pick_by(index, values):
        picked = values[0]
        for i, value in enumerate(values[1:], start=1):
            picked = jnp.where(index == i, value, picked)
        return picked

    def to_experts(got):
        by_shift = [got] + [lax.ppermute(got, "exp", core_shift(s)) for s in range(1, cores)]
        ordered = [pick_by((core - source) % cores, by_shift) for source in range(cores)]
        return jnp.concatenate(
            [ordered[q][:, p * slice_w:(p + 1) * slice_w] for p in range(EXP_DEV) for q in range(cores)],
            axis=1,
        )

    local_slot = route_slots(route_ids, experts, capacity)
    owned = (route_ids % EXP_DEV) == half
    slot_iota = jnp.arange(slots, dtype=jnp.int32)[:, None]
    picks = [
        (local_slot[:, k][None, :] == slot_iota) & owned[:, k][None, :]
        for k in range(route_ids.shape[1])
    ]
    dispatch = picks[0]
    for extra in picks[1:]:
        dispatch = dispatch | extra
    gate_slot = sum(
        jnp.sum(jnp.where(pick, gates[:, k][None, :], 0.0), axis=1) for k, pick in enumerate(picks)
    )
    dispatch_mat = dispatch.astype(bf16)

    def send(buf):
        width = buf.shape[-1]
        return lax.all_to_all(
            buf.reshape(sections, capacity, width), "attn", split_axis=0, concat_axis=0, tiled=True
        ).reshape(slots, width)

    got_own = send(jnp.dot(dispatch_mat, patches, preferred_element_type=f32).astype(bf16))
    x_other = lax.ppermute(patches, "exp", half_swap)
    other_buf = jnp.dot(dispatch_mat, x_other, preferred_element_type=f32).astype(bf16)
    sub_dy = core_subset(grad_out)
    sub_dy, other_buf = lax.optimization_barrier((sub_dy, other_buf))
    got_other = send(other_buf)
    first = half == 0
    got_x = jnp.concatenate(
        [jnp.where(first, got_own, got_other), jnp.where(first, got_other, got_own)], axis=1
    )
    dy_buf = jnp.dot(dispatch_mat, sub_dy, preferred_element_type=f32)
    d_buf = (gate_slot[:, None] * dy_buf).astype(bf16)
    x_rows = to_experts(got_x)
    d_buf, x_rows = lax.optimization_barrier((d_buf, x_rows))
    got_d = send(d_buf)

    if n_loc == 1:
        up_mat = w_up[0]
    else:
        up_mat = jnp.transpose(w_up, (1, 0, 2)).reshape(model_width, n_loc * hid_loc)
    down_mat = w_down.reshape(n_loc * hid_loc, model_width)

    pre_act = jnp.dot(x_rows, up_mat, preferred_element_type=f32)
    gelu_value, gelu_slope = gelu_parts(pre_act)
    activation = gelu_value.astype(bf16)

    out_loc = None
    for g in range(n_loc):
        part = slice(g * hid_loc, (g + 1) * hid_loc)
        out_g = jnp.dot(activation[:, part], w_down[g], preferred_element_type=f32)
        out_g = out_g.astype(bf16).astype(f32)
        out_loc = out_g if out_loc is None else out_loc + out_g

    def group_sum(rows, hold):
        subsets = [
            jnp.concatenate(
                [rows[:, (p * cores + q) * slice_w:(p * cores + q + 1) * slice_w] for p in range(EXP_DEV)],
                axis=1,
            )
            for q in range(cores)
        ]
        summed = pick_by(core, subsets)
        for s in range(1, cores):
            theirs = pick_by((core + s) % cores, subsets)
            got = lax.ppermute(theirs.astype(bf16), "exp", core_shift(s))
            summed = summed + got.astype(f32)
        return lax.optimization_barrier((summed.astype(bf16), hold))

    def finish(sub):
        pieces = [sub[:, p * slice_w:(p + 1) * slice_w] for p in range(EXP_DEV)]
        keep = pick_by(half, pieces)
        give = pick_by((half + 1) % EXP_DEV, pieces)
        return (keep + lax.ppermute(give, "exp", half_swap)).astype(bf16)

    sum_out, got_d = group_sum(out_loc, got_d)
    back_out = send(sum_out)
    d_rows = to_experts(got_d)
    grad_act = jnp.einsum("sd,hd->sh", d_rows, down_mat, preferred_element_type=f32)
    grad_pre = (grad_act * gelu_slope).astype(bf16)
    dx_loc = None
    for g in range(n_loc):
        part = slice(g * hid_loc, (g + 1) * hid_loc)
        dx_g = jnp.einsum("sh,dh->sd", grad_pre[:, part], w_up[g], preferred_element_type=f32)
        dx_g = dx_g.astype(bf16).astype(f32)
        dx_loc = dx_g if dx_loc is None else dx_loc + dx_g
    grad_down = jnp.einsum("sh,sd->hd", activation, d_rows, preferred_element_type=f32)
    sum_dx, (x_late, pre_late, grad_down) = group_sum(dx_loc, (x_rows, grad_pre, grad_down))
    dx_pieces = [sum_dx[:, p * slice_w:(p + 1) * slice_w] for p in range(EXP_DEV)]
    back_give = send(pick_by((half + 1) % EXP_DEV, dx_pieces))
    dx_give = jnp.dot(dispatch_mat.T, back_give, preferred_element_type=f32)
    dx_came = lax.ppermute(dx_give, "exp", half_swap)
    back_keep = send(pick_by(half, dx_pieces))
    dx_give, x_late, pre_late = lax.optimization_barrier((dx_give, x_late, pre_late))
    grad_up = jnp.einsum("sd,sh->dh", x_late, pre_late, preferred_element_type=f32)
    back_keep, grad_up = lax.optimization_barrier((back_keep, grad_up))
    grad_patches = (jnp.dot(dispatch_mat.T, back_keep, preferred_element_type=f32) + dx_came).astype(bf16)

    mixed_sub = None
    for k, pick in enumerate(picks):
        picked = jnp.dot(pick.astype(bf16).T, back_out, preferred_element_type=f32)
        term = gates[:, k][:, None] * picked
        mixed_sub = term if mixed_sub is None else mixed_sub + term
    mixed = finish(mixed_sub)
    grad_up = jnp.transpose(grad_up.reshape(model_width, n_loc, hid_loc), (1, 0, 2))
    grad_down = grad_down.reshape(n_loc, hid_loc, model_width)
    return (mixed, grad_patches, grad_up, grad_down)


def solution(mesh):
    return jax.shard_map(
        on_device,
        mesh=mesh,
        in_specs=(
            P("attn", "exp"),
            P("attn", "exp"),
            P("attn", None),
            P("attn", None),
            P(("attn", "exp"), None, None),
            P(("attn", "exp"), None, None),
        ),
        out_specs=(
            P("attn", "exp"),
            P("attn", "exp"),
            P(("attn", "exp"), None, None),
            P(("attn", "exp"), None, None),
        ),
        check_vma=False,
    )
```

```python
import jax
import jax.numpy as jnp
from jax import lax
from jax.sharding import PartitionSpec as P

EXP_DEV = 2


def gelu_parts(pre_act):
    inner_arg = 0.7978845608 * (pre_act + 0.044715 * pre_act * pre_act * pre_act)
    tanh_val = jnp.tanh(inner_arg)
    gelu_value = 0.5 * pre_act * (1.0 + tanh_val)
    gelu_slope = 0.5 * (1.0 + tanh_val) + 0.5 * pre_act * (
        1.0 - tanh_val * tanh_val
    ) * 0.7978845608 * (1.0 + 0.134145 * pre_act * pre_act)
    return (gelu_value, gelu_slope)


def route_slots(route_ids, experts, capacity):
    flat_ids = route_ids.reshape(-1)
    one_hot = (flat_ids[:, None] == jnp.arange(experts, dtype=jnp.int32)[None, :]).astype(jnp.int32)
    before = jnp.cumsum(one_hot, axis=0) - one_hot
    rank_in = jnp.sum(before * one_hot, axis=1).reshape(route_ids.shape)
    return (route_ids // EXP_DEV) * capacity + rank_in


def on_device(patches, grad_out, route_ids, gates, w_up, w_down):
    sections = lax.axis_size("attn")
    n_exp = lax.axis_size("exp")
    cores = n_exp // EXP_DEV
    me = lax.axis_index("exp")
    half = me // cores
    core = me % cores
    experts = EXP_DEV * sections
    token_count, slice_w = patches.shape
    capacity = 4 * token_count // experts
    slots = sections * capacity
    n_loc, model_width, hid_loc = w_up.shape
    sub_w = EXP_DEV * slice_w
    f32 = jnp.float32
    bf16 = jnp.bfloat16

    def core_shift(s):
        return [(i, (i // cores) * cores + (i % cores + s) % cores) for i in range(n_exp)]

    half_swap = [(i, (i + cores) % n_exp) for i in range(n_exp)]

    def core_subset(local):
        other = lax.ppermute(local, "exp", half_swap)
        first = half == 0
        return jnp.concatenate(
            [jnp.where(first, local, other), jnp.where(first, other, local)], axis=1
        )

    def pick_by(index, values):
        picked = values[0]
        for i, value in enumerate(values[1:], start=1):
            picked = jnp.where(index == i, value, picked)
        return picked

    def to_experts(got):
        by_shift = [got] + [lax.ppermute(got, "exp", core_shift(s)) for s in range(1, cores)]
        ordered = [pick_by((core - source) % cores, by_shift) for source in range(cores)]
        return jnp.concatenate(
            [ordered[q][:, p * slice_w:(p + 1) * slice_w] for p in range(EXP_DEV) for q in range(cores)],
            axis=1,
        )

    local_slot = route_slots(route_ids, experts, capacity)
    owned = (route_ids % EXP_DEV) == half
    slot_iota = jnp.arange(slots, dtype=jnp.int32)[:, None]
    picks = [
        (local_slot[:, k][None, :] == slot_iota) & owned[:, k][None, :]
        for k in range(route_ids.shape[1])
    ]
    dispatch = picks[0]
    for extra in picks[1:]:
        dispatch = dispatch | extra
    gate_slot = sum(
        jnp.sum(jnp.where(pick, gates[:, k][None, :], 0.0), axis=1) for k, pick in enumerate(picks)
    )
    dispatch_mat = dispatch.astype(bf16)

    def send(buf):
        width = buf.shape[-1]
        return lax.all_to_all(
            buf.reshape(sections, capacity, width), "attn", split_axis=0, concat_axis=0, tiled=True
        ).reshape(slots, width)

    got_own = send(jnp.dot(dispatch_mat, patches, preferred_element_type=f32).astype(bf16))
    x_other = lax.ppermute(patches, "exp", half_swap)
    other_buf = jnp.dot(dispatch_mat, x_other, preferred_element_type=f32).astype(bf16)
    sub_dy = core_subset(grad_out)
    sub_dy, other_buf = lax.optimization_barrier((sub_dy, other_buf))
    got_other = send(other_buf)
    dy_buf = jnp.dot(dispatch_mat, sub_dy, preferred_element_type=f32)
    d_buf = (gate_slot[:, None] * dy_buf).astype(bf16)
    own_all = [got_own] + [lax.ppermute(got_own, "exp", core_shift(s)) for s in range(1, cores)]
    other_all = [got_other] + [lax.ppermute(got_other, "exp", core_shift(s)) for s in range(1, cores)]
    x_pieces = []
    for p in range(EXP_DEV):
        for q in range(cores):
            shift = (core - q) % cores
            x_pieces.append(
                jnp.where(p == half, pick_by(shift, own_all), pick_by(shift, other_all))
            )
    x_rows = jnp.concatenate(x_pieces, axis=1)
    d_buf, x_rows = lax.optimization_barrier((d_buf, x_rows))
    got_d = send(d_buf)

    if n_loc == 1:
        up_mat = w_up[0]
    else:
        up_mat = jnp.transpose(w_up, (1, 0, 2)).reshape(model_width, n_loc * hid_loc)
    down_mat = w_down.reshape(n_loc * hid_loc, model_width)

    pre_act = jnp.dot(x_rows, up_mat, preferred_element_type=f32)
    gelu_value, gelu_slope = gelu_parts(pre_act)
    activation = gelu_value.astype(bf16)

    out_loc = None
    for g in range(n_loc):
        part = slice(g * hid_loc, (g + 1) * hid_loc)
        out_g = jnp.dot(activation[:, part], w_down[g], preferred_element_type=f32)
        out_g = out_g.astype(bf16).astype(f32)
        out_loc = out_g if out_loc is None else out_loc + out_g

    def group_sum(rows, hold):
        subsets = [
            jnp.concatenate(
                [rows[:, (p * cores + q) * slice_w:(p * cores + q + 1) * slice_w] for p in range(EXP_DEV)],
                axis=1,
            )
            for q in range(cores)
        ]
        summed = pick_by(core, subsets)
        for s in range(1, cores):
            theirs = pick_by((core + s) % cores, subsets)
            got = lax.ppermute(theirs.astype(bf16), "exp", core_shift(s))
            summed = summed + got.astype(f32)
        return lax.optimization_barrier((summed.astype(bf16), hold))

    def finish(sub):
        pieces = [sub[:, p * slice_w:(p + 1) * slice_w] for p in range(EXP_DEV)]
        keep = pick_by(half, pieces)
        give = pick_by((half + 1) % EXP_DEV, pieces)
        return (keep + lax.ppermute(give, "exp", half_swap)).astype(bf16)

    sum_out, got_d = group_sum(out_loc, got_d)
    back_out = send(sum_out)
    d_rows = to_experts(got_d)
    grad_act = jnp.einsum("sd,hd->sh", d_rows, down_mat, preferred_element_type=f32)
    grad_pre = (grad_act * gelu_slope).astype(bf16)
    dx_loc = None
    for g in range(n_loc):
        part = slice(g * hid_loc, (g + 1) * hid_loc)
        dx_g = jnp.einsum("sh,dh->sd", grad_pre[:, part], w_up[g], preferred_element_type=f32)
        dx_g = dx_g.astype(bf16).astype(f32)
        dx_loc = dx_g if dx_loc is None else dx_loc + dx_g
    grad_down = jnp.einsum("sh,sd->hd", activation, d_rows, preferred_element_type=f32)
    sum_dx, (x_late, pre_late, grad_down) = group_sum(dx_loc, (x_rows, grad_pre, grad_down))
    dx_pieces = [sum_dx[:, p * slice_w:(p + 1) * slice_w] for p in range(EXP_DEV)]
    back_give = send(pick_by((half + 1) % EXP_DEV, dx_pieces))
    dx_give = jnp.dot(dispatch_mat.T, back_give, preferred_element_type=f32)
    dx_came = lax.ppermute(dx_give, "exp", half_swap)
    back_keep = send(pick_by(half, dx_pieces))
    dx_give, x_late, pre_late = lax.optimization_barrier((dx_give, x_late, pre_late))
    grad_up = jnp.einsum("sd,sh->dh", x_late, pre_late, preferred_element_type=f32)
    back_keep, grad_up = lax.optimization_barrier((back_keep, grad_up))
    grad_patches = (jnp.dot(dispatch_mat.T, back_keep, preferred_element_type=f32) + dx_came).astype(bf16)

    mixed_sub = None
    for k, pick in enumerate(picks):
        picked = jnp.dot(pick.astype(bf16).T, back_out, preferred_element_type=f32)
        term = gates[:, k][:, None] * picked
        mixed_sub = term if mixed_sub is None else mixed_sub + term
    mixed = finish(mixed_sub)
    grad_up = jnp.transpose(grad_up.reshape(model_width, n_loc, hid_loc), (1, 0, 2))
    grad_down = grad_down.reshape(n_loc, hid_loc, model_width)
    return (mixed, grad_patches, grad_up, grad_down)


def solution(mesh):
    return jax.shard_map(
        on_device,
        mesh=mesh,
        in_specs=(
            P("attn", "exp"),
            P("attn", "exp"),
            P("attn", None),
            P("attn", None),
            P(("attn", "exp"), None, None),
            P(("attn", "exp"), None, None),
        ),
        out_specs=(
            P("attn", "exp"),
            P("attn", "exp"),
            P(("attn", "exp"), None, None),
            P(("attn", "exp"), None, None),
        ),
        check_vma=False,
    )
```

```python
import jax
import jax.numpy as jnp
from jax import lax
from jax.sharding import PartitionSpec as P

EXP_DEV = 2


def gelu_parts(pre_act):
    inner_arg = 0.7978845608 * (pre_act + 0.044715 * pre_act * pre_act * pre_act)
    tanh_val = jnp.tanh(inner_arg)
    gelu_value = 0.5 * pre_act * (1.0 + tanh_val)
    gelu_slope = 0.5 * (1.0 + tanh_val) + 0.5 * pre_act * (
        1.0 - tanh_val * tanh_val
    ) * 0.7978845608 * (1.0 + 0.134145 * pre_act * pre_act)
    return (gelu_value, gelu_slope)


def route_slots(route_ids, experts, capacity):
    flat_ids = route_ids.reshape(-1)
    one_hot = (flat_ids[:, None] == jnp.arange(experts, dtype=jnp.int32)[None, :]).astype(jnp.int32)
    before = jnp.cumsum(one_hot, axis=0) - one_hot
    rank_in = jnp.sum(before * one_hot, axis=1).reshape(route_ids.shape)
    return (route_ids // EXP_DEV) * capacity + rank_in


def on_device(patches, grad_out, route_ids, gates, w_up, w_down):
    sections = lax.axis_size("attn")
    n_exp = lax.axis_size("exp")
    cores = n_exp // EXP_DEV
    me = lax.axis_index("exp")
    half = me // cores
    core = me % cores
    experts = EXP_DEV * sections
    token_count, slice_w = patches.shape
    capacity = 4 * token_count // experts
    slots = sections * capacity
    n_loc, model_width, hid_loc = w_up.shape
    sub_w = EXP_DEV * slice_w
    f32 = jnp.float32
    bf16 = jnp.bfloat16

    def core_shift(s):
        return [(i, (i // cores) * cores + (i % cores + s) % cores) for i in range(n_exp)]

    half_swap = [(i, (i + cores) % n_exp) for i in range(n_exp)]

    def core_subset(local):
        other = lax.ppermute(local, "exp", half_swap)
        first = half == 0
        return jnp.concatenate(
            [jnp.where(first, local, other), jnp.where(first, other, local)], axis=1
        )

    def pick_by(index, values):
        picked = values[0]
        for i, value in enumerate(values[1:], start=1):
            picked = jnp.where(index == i, value, picked)
        return picked

    def to_experts(got):
        by_shift = [got] + [lax.ppermute(got, "exp", core_shift(s)) for s in range(1, cores)]
        ordered = [pick_by((core - source) % cores, by_shift) for source in range(cores)]
        return jnp.concatenate(
            [ordered[q][:, p * slice_w:(p + 1) * slice_w] for p in range(EXP_DEV) for q in range(cores)],
            axis=1,
        )

    local_slot = route_slots(route_ids, experts, capacity)
    owned = (route_ids % EXP_DEV) == half
    slot_iota = jnp.arange(slots, dtype=jnp.int32)[:, None]
    picks = [
        (local_slot[:, k][None, :] == slot_iota) & owned[:, k][None, :]
        for k in range(route_ids.shape[1])
    ]
    dispatch = picks[0]
    for extra in picks[1:]:
        dispatch = dispatch | extra
    gate_slot = sum(
        jnp.sum(jnp.where(pick, gates[:, k][None, :], 0.0), axis=1) for k, pick in enumerate(picks)
    )
    dispatch_mat = dispatch.astype(bf16)
    picks_other = [
        (local_slot[:, k][None, :] == slot_iota) & ~owned[:, k][None, :]
        for k in range(route_ids.shape[1])
    ]
    dispatch_other = picks_other[0]
    for extra in picks_other[1:]:
        dispatch_other = dispatch_other | extra
    dispatch_other_mat = dispatch_other.astype(bf16)

    def send(buf):
        width = buf.shape[-1]
        return lax.all_to_all(
            buf.reshape(sections, capacity, width), "attn", split_axis=0, concat_axis=0, tiled=True
        ).reshape(slots, width)

    got_own = send(jnp.dot(dispatch_mat, patches, preferred_element_type=f32).astype(bf16))
    x_other = lax.ppermute(patches, "exp", half_swap)
    other_buf = jnp.dot(dispatch_mat, x_other, preferred_element_type=f32).astype(bf16)
    sub_dy = core_subset(grad_out)
    sub_dy, other_buf = lax.optimization_barrier((sub_dy, other_buf))
    got_other = send(other_buf)
    dy_buf = jnp.dot(dispatch_mat, sub_dy, preferred_element_type=f32)
    d_buf = (gate_slot[:, None] * dy_buf).astype(bf16)
    own_all = [got_own] + [lax.ppermute(got_own, "exp", core_shift(s)) for s in range(1, cores)]
    other_all = [got_other] + [lax.ppermute(got_other, "exp", core_shift(s)) for s in range(1, cores)]
    x_pieces = []
    for p in range(EXP_DEV):
        for q in range(cores):
            shift = (core - q) % cores
            x_pieces.append(
                jnp.where(p == half, pick_by(shift, own_all), pick_by(shift, other_all))
            )
    x_rows = jnp.concatenate(x_pieces, axis=1)
    d_buf, x_rows = lax.optimization_barrier((d_buf, x_rows))
    got_d = send(d_buf)

    if n_loc == 1:
        up_mat = w_up[0]
    else:
        up_mat = jnp.transpose(w_up, (1, 0, 2)).reshape(model_width, n_loc * hid_loc)
    down_mat = w_down.reshape(n_loc * hid_loc, model_width)

    pre_act = jnp.dot(x_rows, up_mat, preferred_element_type=f32)
    gelu_value, gelu_slope = gelu_parts(pre_act)
    activation = gelu_value.astype(bf16)

    out_loc = None
    for g in range(n_loc):
        part = slice(g * hid_loc, (g + 1) * hid_loc)
        out_g = jnp.dot(activation[:, part], w_down[g], preferred_element_type=f32)
        out_g = out_g.astype(bf16).astype(f32)
        out_loc = out_g if out_loc is None else out_loc + out_g

    def group_sum(rows, hold):
        subsets = [
            jnp.concatenate(
                [rows[:, (p * cores + q) * slice_w:(p * cores + q + 1) * slice_w] for p in range(EXP_DEV)],
                axis=1,
            )
            for q in range(cores)
        ]
        summed = pick_by(core, subsets)
        for s in range(1, cores):
            theirs = pick_by((core + s) % cores, subsets)
            got = lax.ppermute(theirs.astype(bf16), "exp", core_shift(s))
            summed = summed + got.astype(f32)
        return lax.optimization_barrier((summed.astype(bf16), hold))

    def to_sections(summed, hold=()):
        pieces = [summed[:, p * slice_w:(p + 1) * slice_w] for p in range(EXP_DEV)]
        keep = pick_by(half, pieces)
        give = lax.ppermute(pick_by((half + 1) % EXP_DEV, pieces), "exp", half_swap)
        payload, hold = lax.optimization_barrier((jnp.concatenate([keep, give], axis=1), hold))
        back = send(payload)
        return back[:, :slice_w], back[:, slice_w:], hold

    sum_out, got_d = group_sum(out_loc, got_d)
    out_keep, out_give, _ = to_sections(sum_out)
    d_rows = to_experts(got_d)
    grad_act = jnp.einsum("sd,hd->sh", d_rows, down_mat, preferred_element_type=f32)
    grad_pre = (grad_act * gelu_slope).astype(bf16)
    dx_loc = None
    for g in range(n_loc):
        part = slice(g * hid_loc, (g + 1) * hid_loc)
        dx_g = jnp.einsum("sh,dh->sd", grad_pre[:, part], w_up[g], preferred_element_type=f32)
        dx_g = dx_g.astype(bf16).astype(f32)
        dx_loc = dx_g if dx_loc is None else dx_loc + dx_g
    sum_dx, late = group_sum(dx_loc, (activation, d_rows, x_rows, grad_pre))
    dx_keep, dx_give, late = to_sections(sum_dx, late)
    act_late, d_late, x_late, pre_late = late
    grad_down = jnp.einsum("sh,sd->hd", act_late, d_late, preferred_element_type=f32)
    grad_up = jnp.einsum("sd,sh->dh", x_late, pre_late, preferred_element_type=f32)

    mixed = None
    for k in range(len(picks)):
        picked = jnp.dot(picks[k].astype(bf16).T, out_keep, preferred_element_type=f32)
        picked = picked + jnp.dot(picks_other[k].astype(bf16).T, out_give, preferred_element_type=f32)
        term = gates[:, k][:, None] * picked
        mixed = term if mixed is None else mixed + term
    mixed = mixed.astype(bf16)
    dx_keep, dx_give, grad_up, grad_down = lax.optimization_barrier((dx_keep, dx_give, grad_up, grad_down))
    grad_patches = (
        jnp.dot(dispatch_mat.T, dx_keep, preferred_element_type=f32)
        + jnp.dot(dispatch_other_mat.T, dx_give, preferred_element_type=f32)
    ).astype(bf16)
    grad_up = jnp.transpose(grad_up.reshape(model_width, n_loc, hid_loc), (1, 0, 2))
    grad_down = grad_down.reshape(n_loc, hid_loc, model_width)
    return (mixed, grad_patches, grad_up, grad_down)


def solution(mesh):
    return jax.shard_map(
        on_device,
        mesh=mesh,
        in_specs=(
            P("attn", "exp"),
            P("attn", "exp"),
            P("attn", None),
            P("attn", None),
            P(("attn", "exp"), None, None),
            P(("attn", "exp"), None, None),
        ),
        out_specs=(
            P("attn", "exp"),
            P("attn", "exp"),
            P(("attn", "exp"), None, None),
            P(("attn", "exp"), None, None),
        ),
        check_vma=False,
    )
```

```python
import jax
import jax.numpy as jnp
from jax import lax
from jax.sharding import PartitionSpec as P

EXP_DEV = 2


def gelu_parts(pre_act):
    inner_arg = 0.7978845608 * (pre_act + 0.044715 * pre_act * pre_act * pre_act)
    tanh_val = jnp.tanh(inner_arg)
    gelu_value = 0.5 * pre_act * (1.0 + tanh_val)
    gelu_slope = 0.5 * (1.0 + tanh_val) + 0.5 * pre_act * (
        1.0 - tanh_val * tanh_val
    ) * 0.7978845608 * (1.0 + 0.134145 * pre_act * pre_act)
    return (gelu_value, gelu_slope)


def route_slots(route_ids, experts, capacity):
    flat_ids = route_ids.reshape(-1)
    one_hot = (flat_ids[:, None] == jnp.arange(experts, dtype=jnp.int32)[None, :]).astype(jnp.int32)
    before = jnp.cumsum(one_hot, axis=0) - one_hot
    rank_in = jnp.sum(before * one_hot, axis=1).reshape(route_ids.shape)
    return (route_ids // EXP_DEV) * capacity + rank_in


def on_device(patches, grad_out, route_ids, gates, w_up, w_down):
    sections = lax.axis_size("attn")
    n_exp = lax.axis_size("exp")
    cores = n_exp // EXP_DEV
    me = lax.axis_index("exp")
    half = me // cores
    core = me % cores
    experts = EXP_DEV * sections
    token_count, slice_w = patches.shape
    capacity = 4 * token_count // experts
    slots = sections * capacity
    n_loc, model_width, hid_loc = w_up.shape
    sub_w = EXP_DEV * slice_w
    f32 = jnp.float32
    bf16 = jnp.bfloat16

    def core_shift(s):
        return [(i, (i // cores) * cores + (i % cores + s) % cores) for i in range(n_exp)]

    half_swap = [(i, (i + cores) % n_exp) for i in range(n_exp)]

    def pick_by(index, values):
        picked = values[0]
        for i, value in enumerate(values[1:], start=1):
            picked = jnp.where(index == i, value, picked)
        return picked

    def to_experts(got):
        by_shift = [got] + [lax.ppermute(got, "exp", core_shift(s)) for s in range(1, cores)]
        ordered = [pick_by((core - source) % cores, by_shift) for source in range(cores)]
        return jnp.concatenate(
            [ordered[q][:, p * slice_w:(p + 1) * slice_w] for p in range(EXP_DEV) for q in range(cores)],
            axis=1,
        )

    local_slot = route_slots(route_ids, experts, capacity)
    owned = (route_ids % EXP_DEV) == half
    slot_iota = jnp.arange(slots, dtype=jnp.int32)[:, None]
    picks = [
        (local_slot[:, k][None, :] == slot_iota) & owned[:, k][None, :]
        for k in range(route_ids.shape[1])
    ]
    dispatch = picks[0]
    for extra in picks[1:]:
        dispatch = dispatch | extra
    gate_slot = sum(
        jnp.sum(jnp.where(pick, gates[:, k][None, :], 0.0), axis=1) for k, pick in enumerate(picks)
    )
    dispatch_mat = dispatch.astype(bf16)

    def send(buf):
        width = buf.shape[-1]
        return lax.all_to_all(
            buf.reshape(sections, capacity, width), "attn", split_axis=0, concat_axis=0, tiled=True
        ).reshape(slots, width)

    got_own = send(jnp.dot(dispatch_mat, patches, preferred_element_type=f32).astype(bf16))
    both_other = lax.ppermute(jnp.concatenate([patches, grad_out], axis=1), "exp", half_swap)
    x_other = both_other[:, :slice_w]
    dy_other = both_other[:, slice_w:]
    other_buf = jnp.dot(dispatch_mat, x_other, preferred_element_type=f32).astype(bf16)
    sub_dy = jnp.concatenate(
        [jnp.where(half == 0, grad_out, dy_other), jnp.where(half == 0, dy_other, grad_out)], axis=1
    )
    sub_dy, other_buf = lax.optimization_barrier((sub_dy, other_buf))
    got_other = send(other_buf)
    dy_buf = jnp.dot(dispatch_mat, sub_dy, preferred_element_type=f32)
    d_buf = (gate_slot[:, None] * dy_buf).astype(bf16)
    own_all = [got_own] + [lax.ppermute(got_own, "exp", core_shift(s)) for s in range(1, cores)]
    other_all = [got_other] + [lax.ppermute(got_other, "exp", core_shift(s)) for s in range(1, cores)]
    x_pieces = []
    for p in range(EXP_DEV):
        for q in range(cores):
            shift = (core - q) % cores
            x_pieces.append(
                jnp.where(p == half, pick_by(shift, own_all), pick_by(shift, other_all))
            )
    x_rows = jnp.concatenate(x_pieces, axis=1)
    d_buf, x_rows = lax.optimization_barrier((d_buf, x_rows))
    got_d = send(d_buf)

    if n_loc == 1:
        up_mat = w_up[0]
    else:
        up_mat = jnp.transpose(w_up, (1, 0, 2)).reshape(model_width, n_loc * hid_loc)
    down_mat = w_down.reshape(n_loc * hid_loc, model_width)

    pre_act = jnp.dot(x_rows, up_mat, preferred_element_type=f32)
    gelu_value, gelu_slope = gelu_parts(pre_act)
    activation = gelu_value.astype(bf16)

    out_loc = None
    for g in range(n_loc):
        part = slice(g * hid_loc, (g + 1) * hid_loc)
        out_g = jnp.dot(activation[:, part], w_down[g], preferred_element_type=f32)
        out_g = out_g.astype(bf16).astype(f32)
        out_loc = out_g if out_loc is None else out_loc + out_g

    def group_sum(rows, hold):
        subsets = [
            jnp.concatenate(
                [rows[:, (p * cores + q) * slice_w:(p * cores + q + 1) * slice_w] for p in range(EXP_DEV)],
                axis=1,
            )
            for q in range(cores)
        ]
        summed = pick_by(core, subsets)
        for s in range(1, cores):
            theirs = pick_by((core + s) % cores, subsets)
            got = lax.ppermute(theirs.astype(bf16), "exp", core_shift(s))
            summed = summed + got.astype(f32)
        return lax.optimization_barrier((summed.astype(bf16), hold))

    def finish(sub):
        pieces = [sub[:, p * slice_w:(p + 1) * slice_w] for p in range(EXP_DEV)]
        keep = pick_by(half, pieces)
        give = pick_by((half + 1) % EXP_DEV, pieces)
        return (keep + lax.ppermute(give, "exp", half_swap)).astype(bf16)

    sum_out, got_d = group_sum(out_loc, got_d)
    back_out = send(sum_out)
    d_rows = to_experts(got_d)
    grad_act = jnp.einsum("sd,hd->sh", d_rows, down_mat, preferred_element_type=f32)
    grad_pre = (grad_act * gelu_slope).astype(bf16)
    dx_loc = None
    for g in range(n_loc):
        part = slice(g * hid_loc, (g + 1) * hid_loc)
        dx_g = jnp.einsum("sh,dh->sd", grad_pre[:, part], w_up[g], preferred_element_type=f32)
        dx_g = dx_g.astype(bf16).astype(f32)
        dx_loc = dx_g if dx_loc is None else dx_loc + dx_g
    grad_down = jnp.einsum("sh,sd->hd", activation, d_rows, preferred_element_type=f32)
    sum_dx, (x_late, pre_late, grad_down) = group_sum(dx_loc, (x_rows, grad_pre, grad_down))
    dx_pieces = [sum_dx[:, p * slice_w:(p + 1) * slice_w] for p in range(EXP_DEV)]
    back_give = send(pick_by((half + 1) % EXP_DEV, dx_pieces))
    dx_give = jnp.dot(dispatch_mat.T, back_give, preferred_element_type=f32)
    dx_came = lax.ppermute(dx_give, "exp", half_swap)
    back_keep = send(pick_by(half, dx_pieces))
    dx_give, x_late, pre_late = lax.optimization_barrier((dx_give, x_late, pre_late))
    grad_up = jnp.einsum("sd,sh->dh", x_late, pre_late, preferred_element_type=f32)
    back_keep, grad_up = lax.optimization_barrier((back_keep, grad_up))
    grad_patches = (jnp.dot(dispatch_mat.T, back_keep, preferred_element_type=f32) + dx_came).astype(bf16)

    mixed_sub = None
    for k, pick in enumerate(picks):
        picked = jnp.dot(pick.astype(bf16).T, back_out, preferred_element_type=f32)
        term = gates[:, k][:, None] * picked
        mixed_sub = term if mixed_sub is None else mixed_sub + term
    mixed = finish(mixed_sub)
    grad_up = jnp.transpose(grad_up.reshape(model_width, n_loc, hid_loc), (1, 0, 2))
    grad_down = grad_down.reshape(n_loc, hid_loc, model_width)
    return (mixed, grad_patches, grad_up, grad_down)


def solution(mesh):
    return jax.shard_map(
        on_device,
        mesh=mesh,
        in_specs=(
            P("attn", "exp"),
            P("attn", "exp"),
            P("attn", None),
            P("attn", None),
            P(("attn", "exp"), None, None),
            P(("attn", "exp"), None, None),
        ),
        out_specs=(
            P("attn", "exp"),
            P("attn", "exp"),
            P(("attn", "exp"), None, None),
            P(("attn", "exp"), None, None),
        ),
        check_vma=False,
    )
```

```python
import jax
import jax.numpy as jnp
from jax import lax
from jax.sharding import PartitionSpec as P

EXP_DEV = 2


def gelu_parts(pre_act):
    inner_arg = 0.7978845608 * (pre_act + 0.044715 * pre_act * pre_act * pre_act)
    tanh_val = jnp.tanh(inner_arg)
    gelu_value = 0.5 * pre_act * (1.0 + tanh_val)
    gelu_slope = 0.5 * (1.0 + tanh_val) + 0.5 * pre_act * (
        1.0 - tanh_val * tanh_val
    ) * 0.7978845608 * (1.0 + 0.134145 * pre_act * pre_act)
    return (gelu_value, gelu_slope)


def route_slots(route_ids, experts, capacity):
    flat_ids = route_ids.reshape(-1)
    one_hot = (flat_ids[:, None] == jnp.arange(experts, dtype=jnp.int32)[None, :]).astype(jnp.int32)
    before = jnp.cumsum(one_hot, axis=0) - one_hot
    rank_in = jnp.sum(before * one_hot, axis=1).reshape(route_ids.shape)
    return (route_ids // EXP_DEV) * capacity + rank_in


def on_device(patches, grad_out, route_ids, gates, w_up, w_down):
    sections = lax.axis_size("attn")
    n_exp = lax.axis_size("exp")
    cores = n_exp // EXP_DEV
    me = lax.axis_index("exp")
    half = me // cores
    core = me % cores
    experts = EXP_DEV * sections
    token_count, slice_w = patches.shape
    capacity = 4 * token_count // experts
    slots = sections * capacity
    n_loc, model_width, hid_loc = w_up.shape
    sub_w = EXP_DEV * slice_w
    f32 = jnp.float32
    bf16 = jnp.bfloat16

    def core_shift(s):
        return [(i, (i // cores) * cores + (i % cores + s) % cores) for i in range(n_exp)]

    half_swap = [(i, (i + cores) % n_exp) for i in range(n_exp)]

    def pick_by(index, values):
        picked = values[0]
        for i, value in enumerate(values[1:], start=1):
            picked = jnp.where(index == i, value, picked)
        return picked

    def to_experts(got):
        by_shift = [got] + [lax.ppermute(got, "exp", core_shift(s)) for s in range(1, cores)]
        ordered = [pick_by((core - source) % cores, by_shift) for source in range(cores)]
        return jnp.concatenate(
            [ordered[q][:, p * slice_w:(p + 1) * slice_w] for p in range(EXP_DEV) for q in range(cores)],
            axis=1,
        )

    local_slot = route_slots(route_ids, experts, capacity)
    owned = (route_ids % EXP_DEV) == half
    slot_iota = jnp.arange(slots, dtype=jnp.int32)[:, None]
    picks = [
        (local_slot[:, k][None, :] == slot_iota) & owned[:, k][None, :]
        for k in range(route_ids.shape[1])
    ]
    dispatch = picks[0]
    for extra in picks[1:]:
        dispatch = dispatch | extra
    gate_slot = sum(
        jnp.sum(jnp.where(pick, gates[:, k][None, :], 0.0), axis=1) for k, pick in enumerate(picks)
    )
    dispatch_mat = dispatch.astype(bf16)

    def send(buf):
        width = buf.shape[-1]
        return lax.all_to_all(
            buf.reshape(sections, capacity, width), "attn", split_axis=0, concat_axis=0, tiled=True
        ).reshape(slots, width)

    got_own = send(jnp.dot(dispatch_mat, patches, preferred_element_type=f32).astype(bf16))
    both_other = lax.ppermute(jnp.concatenate([patches, grad_out], axis=1), "exp", half_swap)
    x_other = both_other[:, :slice_w]
    dy_other = both_other[:, slice_w:]
    other_buf = jnp.dot(dispatch_mat, x_other, preferred_element_type=f32).astype(bf16)
    sub_dy = jnp.concatenate(
        [jnp.where(half == 0, grad_out, dy_other), jnp.where(half == 0, dy_other, grad_out)], axis=1
    )
    dy_buf = jnp.dot(dispatch_mat, sub_dy, preferred_element_type=f32)
    d_buf = (gate_slot[:, None] * dy_buf).astype(bf16)
    d_buf, other_buf = lax.optimization_barrier((d_buf, other_buf))
    got_other = send(other_buf)
    own_all = [got_own] + [lax.ppermute(got_own, "exp", core_shift(s)) for s in range(1, cores)]
    other_all = [got_other] + [lax.ppermute(got_other, "exp", core_shift(s)) for s in range(1, cores)]
    x_pieces = []
    for p in range(EXP_DEV):
        for q in range(cores):
            shift = (core - q) % cores
            x_pieces.append(
                jnp.where(p == half, pick_by(shift, own_all), pick_by(shift, other_all))
            )
    x_rows = jnp.concatenate(x_pieces, axis=1)
    d_buf, x_rows = lax.optimization_barrier((d_buf, x_rows))
    got_d = send(d_buf)

    if n_loc == 1:
        up_mat = w_up[0]
    else:
        up_mat = jnp.transpose(w_up, (1, 0, 2)).reshape(model_width, n_loc * hid_loc)
    down_mat = w_down.reshape(n_loc * hid_loc, model_width)

    pre_act = jnp.dot(x_rows, up_mat, preferred_element_type=f32)
    gelu_value, gelu_slope = gelu_parts(pre_act)
    activation = gelu_value.astype(bf16)

    out_loc = None
    for g in range(n_loc):
        part = slice(g * hid_loc, (g + 1) * hid_loc)
        out_g = jnp.dot(activation[:, part], w_down[g], preferred_element_type=f32)
        out_g = out_g.astype(bf16).astype(f32)
        out_loc = out_g if out_loc is None else out_loc + out_g

    def group_sum(rows, hold):
        subsets = [
            jnp.concatenate(
                [rows[:, (p * cores + q) * slice_w:(p * cores + q + 1) * slice_w] for p in range(EXP_DEV)],
                axis=1,
            )
            for q in range(cores)
        ]
        summed = pick_by(core, subsets)
        for s in range(1, cores):
            theirs = pick_by((core + s) % cores, subsets)
            got = lax.ppermute(theirs.astype(bf16), "exp", core_shift(s))
            summed = summed + got.astype(f32)
        return lax.optimization_barrier((summed.astype(bf16), hold))

    def finish(sub):
        pieces = [sub[:, p * slice_w:(p + 1) * slice_w] for p in range(EXP_DEV)]
        keep = pick_by(half, pieces)
        give = pick_by((half + 1) % EXP_DEV, pieces)
        return (keep + lax.ppermute(give, "exp", half_swap)).astype(bf16)

    sum_out, got_d = group_sum(out_loc, got_d)
    back_out = send(sum_out)
    d_rows = to_experts(got_d)
    grad_act = jnp.einsum("sd,hd->sh", d_rows, down_mat, preferred_element_type=f32)
    grad_pre = (grad_act * gelu_slope).astype(bf16)
    dx_loc = None
    for g in range(n_loc):
        part = slice(g * hid_loc, (g + 1) * hid_loc)
        dx_g = jnp.einsum("sh,dh->sd", grad_pre[:, part], w_up[g], preferred_element_type=f32)
        dx_g = dx_g.astype(bf16).astype(f32)
        dx_loc = dx_g if dx_loc is None else dx_loc + dx_g
    grad_down = jnp.einsum("sh,sd->hd", activation, d_rows, preferred_element_type=f32)
    sum_dx, (x_late, pre_late, grad_down) = group_sum(dx_loc, (x_rows, grad_pre, grad_down))
    dx_pieces = [sum_dx[:, p * slice_w:(p + 1) * slice_w] for p in range(EXP_DEV)]
    back_give = send(pick_by((half + 1) % EXP_DEV, dx_pieces))
    dx_give = jnp.dot(dispatch_mat.T, back_give, preferred_element_type=f32)
    dx_came = lax.ppermute(dx_give, "exp", half_swap)
    back_keep = send(pick_by(half, dx_pieces))
    dx_give, x_late, pre_late = lax.optimization_barrier((dx_give, x_late, pre_late))
    grad_up = jnp.einsum("sd,sh->dh", x_late, pre_late, preferred_element_type=f32)
    back_keep, grad_up = lax.optimization_barrier((back_keep, grad_up))
    grad_patches = (jnp.dot(dispatch_mat.T, back_keep, preferred_element_type=f32) + dx_came).astype(bf16)

    mixed_sub = None
    for k, pick in enumerate(picks):
        picked = jnp.dot(pick.astype(bf16).T, back_out, preferred_element_type=f32)
        term = gates[:, k][:, None] * picked
        mixed_sub = term if mixed_sub is None else mixed_sub + term
    mixed = finish(mixed_sub)
    grad_up = jnp.transpose(grad_up.reshape(model_width, n_loc, hid_loc), (1, 0, 2))
    grad_down = grad_down.reshape(n_loc, hid_loc, model_width)
    return (mixed, grad_patches, grad_up, grad_down)


def solution(mesh):
    return jax.shard_map(
        on_device,
        mesh=mesh,
        in_specs=(
            P("attn", "exp"),
            P("attn", "exp"),
            P("attn", None),
            P("attn", None),
            P(("attn", "exp"), None, None),
            P(("attn", "exp"), None, None),
        ),
        out_specs=(
            P("attn", "exp"),
            P("attn", "exp"),
            P(("attn", "exp"), None, None),
            P(("attn", "exp"), None, None),
        ),
        check_vma=False,
    )
```

```python
import jax
import jax.numpy as jnp
from jax import lax
from jax.sharding import PartitionSpec as P

EXP_DEV = 2


def gelu_parts(pre_act):
    inner_arg = 0.7978845608 * (pre_act + 0.044715 * pre_act * pre_act * pre_act)
    tanh_val = jnp.tanh(inner_arg)
    gelu_value = 0.5 * pre_act * (1.0 + tanh_val)
    gelu_slope = 0.5 * (1.0 + tanh_val) + 0.5 * pre_act * (
        1.0 - tanh_val * tanh_val
    ) * 0.7978845608 * (1.0 + 0.134145 * pre_act * pre_act)
    return (gelu_value, gelu_slope)


def route_slots(route_ids, experts, capacity):
    flat_ids = route_ids.reshape(-1)
    one_hot = (flat_ids[:, None] == jnp.arange(experts, dtype=jnp.int32)[None, :]).astype(jnp.int32)
    before = jnp.cumsum(one_hot, axis=0) - one_hot
    rank_in = jnp.sum(before * one_hot, axis=1).reshape(route_ids.shape)
    return (route_ids // EXP_DEV) * capacity + rank_in


def on_device(patches, grad_out, route_ids, gates, w_up, w_down):
    sections = lax.axis_size("attn")
    n_exp = lax.axis_size("exp")
    cores = n_exp // EXP_DEV
    me = lax.axis_index("exp")
    half = me // cores
    core = me % cores
    experts = EXP_DEV * sections
    token_count, slice_w = patches.shape
    capacity = 4 * token_count // experts
    slots = sections * capacity
    n_loc, model_width, hid_loc = w_up.shape
    sub_w = EXP_DEV * slice_w
    f32 = jnp.float32
    bf16 = jnp.bfloat16

    def core_shift(s):
        return [(i, (i // cores) * cores + (i % cores + s) % cores) for i in range(n_exp)]

    half_swap = [(i, (i + cores) % n_exp) for i in range(n_exp)]

    def pick_by(index, values):
        picked = values[0]
        for i, value in enumerate(values[1:], start=1):
            picked = jnp.where(index == i, value, picked)
        return picked

    def to_experts(got):
        by_shift = [got] + [lax.ppermute(got, "exp", core_shift(s)) for s in range(1, cores)]
        ordered = [pick_by((core - source) % cores, by_shift) for source in range(cores)]
        return jnp.concatenate(
            [ordered[q][:, p * slice_w:(p + 1) * slice_w] for p in range(EXP_DEV) for q in range(cores)],
            axis=1,
        )

    local_slot = route_slots(route_ids, experts, capacity)
    owned = (route_ids % EXP_DEV) == half
    slot_iota = jnp.arange(slots, dtype=jnp.int32)[:, None]
    picks = [
        (local_slot[:, k][None, :] == slot_iota) & owned[:, k][None, :]
        for k in range(route_ids.shape[1])
    ]
    dispatch = picks[0]
    for extra in picks[1:]:
        dispatch = dispatch | extra
    gate_slot = sum(
        jnp.sum(jnp.where(pick, gates[:, k][None, :], 0.0), axis=1) for k, pick in enumerate(picks)
    )
    dispatch_mat = dispatch.astype(bf16)

    def send(buf):
        width = buf.shape[-1]
        return lax.all_to_all(
            buf.reshape(sections, capacity, width), "attn", split_axis=0, concat_axis=0, tiled=True
        ).reshape(slots, width)

    got_own = send(jnp.dot(dispatch_mat, patches, preferred_element_type=f32).astype(bf16))
    both_other = lax.ppermute(jnp.concatenate([patches, grad_out], axis=1), "exp", half_swap)
    x_other = both_other[:, :slice_w]
    dy_other = both_other[:, slice_w:]
    other_buf = jnp.dot(dispatch_mat, x_other, preferred_element_type=f32).astype(bf16)
    sub_dy = jnp.concatenate(
        [jnp.where(half == 0, grad_out, dy_other), jnp.where(half == 0, dy_other, grad_out)], axis=1
    )
    dy_buf = jnp.dot(dispatch_mat, sub_dy, preferred_element_type=f32)
    d_buf = (gate_slot[:, None] * dy_buf).astype(bf16)
    d_buf, other_buf = lax.optimization_barrier((d_buf, other_buf))
    got_other = send(other_buf)
    own_all = [got_own] + [lax.ppermute(got_own, "exp", core_shift(s)) for s in range(1, cores)]
    other_all = [got_other] + [lax.ppermute(got_other, "exp", core_shift(s)) for s in range(1, cores)]
    x_pieces = []
    for p in range(EXP_DEV):
        for q in range(cores):
            shift = (core - q) % cores
            x_pieces.append(
                jnp.where(p == half, pick_by(shift, own_all), pick_by(shift, other_all))
            )
    x_rows = jnp.concatenate(x_pieces, axis=1)
    got_d = send(d_buf)

    if n_loc == 1:
        up_mat = w_up[0]
    else:
        up_mat = jnp.transpose(w_up, (1, 0, 2)).reshape(model_width, n_loc * hid_loc)
    down_mat = w_down.reshape(n_loc * hid_loc, model_width)

    pre_act = jnp.dot(x_rows, up_mat, preferred_element_type=f32)
    gelu_value, gelu_slope = gelu_parts(pre_act)
    activation = gelu_value.astype(bf16)

    out_loc = None
    for g in range(n_loc):
        part = slice(g * hid_loc, (g + 1) * hid_loc)
        out_g = jnp.dot(activation[:, part], w_down[g], preferred_element_type=f32)
        out_g = out_g.astype(bf16).astype(f32)
        out_loc = out_g if out_loc is None else out_loc + out_g

    def group_sum(rows, hold):
        subsets = [
            jnp.concatenate(
                [rows[:, (p * cores + q) * slice_w:(p * cores + q + 1) * slice_w] for p in range(EXP_DEV)],
                axis=1,
            )
            for q in range(cores)
        ]
        summed = pick_by(core, subsets)
        for s in range(1, cores):
            theirs = pick_by((core + s) % cores, subsets)
            got = lax.ppermute(theirs.astype(bf16), "exp", core_shift(s))
            summed = summed + got.astype(f32)
        return lax.optimization_barrier((summed.astype(bf16), hold))

    def finish(sub):
        pieces = [sub[:, p * slice_w:(p + 1) * slice_w] for p in range(EXP_DEV)]
        keep = pick_by(half, pieces)
        give = pick_by((half + 1) % EXP_DEV, pieces)
        return (keep + lax.ppermute(give, "exp", half_swap)).astype(bf16)

    sum_out, got_d = group_sum(out_loc, got_d)
    back_out = send(sum_out)
    d_rows = to_experts(got_d)
    grad_act = jnp.einsum("sd,hd->sh", d_rows, down_mat, preferred_element_type=f32)
    grad_pre = (grad_act * gelu_slope).astype(bf16)
    dx_loc = None
    for g in range(n_loc):
        part = slice(g * hid_loc, (g + 1) * hid_loc)
        dx_g = jnp.einsum("sh,dh->sd", grad_pre[:, part], w_up[g], preferred_element_type=f32)
        dx_g = dx_g.astype(bf16).astype(f32)
        dx_loc = dx_g if dx_loc is None else dx_loc + dx_g
    grad_down = jnp.einsum("sh,sd->hd", activation, d_rows, preferred_element_type=f32)
    sum_dx, (x_late, pre_late, grad_down) = group_sum(dx_loc, (x_rows, grad_pre, grad_down))
    dx_pieces = [sum_dx[:, p * slice_w:(p + 1) * slice_w] for p in range(EXP_DEV)]
    back_give = send(pick_by((half + 1) % EXP_DEV, dx_pieces))
    dx_give = jnp.dot(dispatch_mat.T, back_give, preferred_element_type=f32)
    dx_came = lax.ppermute(dx_give, "exp", half_swap)
    back_keep = send(pick_by(half, dx_pieces))
    dx_give, x_late, pre_late = lax.optimization_barrier((dx_give, x_late, pre_late))
    grad_up = jnp.einsum("sd,sh->dh", x_late, pre_late, preferred_element_type=f32)
    back_keep, grad_up = lax.optimization_barrier((back_keep, grad_up))
    grad_patches = (jnp.dot(dispatch_mat.T, back_keep, preferred_element_type=f32) + dx_came).astype(bf16)

    mixed_sub = None
    for k, pick in enumerate(picks):
        picked = jnp.dot(pick.astype(bf16).T, back_out, preferred_element_type=f32)
        term = gates[:, k][:, None] * picked
        mixed_sub = term if mixed_sub is None else mixed_sub + term
    mixed = finish(mixed_sub)
    grad_up = jnp.transpose(grad_up.reshape(model_width, n_loc, hid_loc), (1, 0, 2))
    grad_down = grad_down.reshape(n_loc, hid_loc, model_width)
    return (mixed, grad_patches, grad_up, grad_down)


def solution(mesh):
    return jax.shard_map(
        on_device,
        mesh=mesh,
        in_specs=(
            P("attn", "exp"),
            P("attn", "exp"),
            P("attn", None),
            P("attn", None),
            P(("attn", "exp"), None, None),
            P(("attn", "exp"), None, None),
        ),
        out_specs=(
            P("attn", "exp"),
            P("attn", "exp"),
            P(("attn", "exp"), None, None),
            P(("attn", "exp"), None, None),
        ),
        check_vma=False,
    )
```
